32 devices in a mesh: groups: 2 (over y), ctx: 4 (over z), head: 4 (over x, core).
Axes of the slice: x: 2, y: 2, z: 4, core: 2. Of those that a mesh axis runs over, the one named last changes fastest.
Arguments:
- query_nope: bfloat16 [16, 128, 128], P('groups', 'head'), parts along dimension 0, may hold values from -9 to 9
- query_rope: bfloat16 [16, 128, 64], P('groups', 'head'), parts along dimension 0, may hold values from -500 to 500
- kv_cache: bfloat16 [8, 2048, 576], P('groups', 'ctx'), parts along dimension 0, may hold values from -8 to 8
- lengths: int32 [8], P('groups'), parts along dimension 0, may hold values from 2 to 2048, as said below
- w_absorb: bfloat16 [128, 128, 512], P('head', None, 'ctx'), may hold values from -0.5 to 0.5
- w_value: bfloat16 [128, 512, 128], P('head', 'ctx'), may hold values from -0.25 to 0.25
- w_output: bfloat16 [16384, 7168], P('head', 'ctx'), may hold values from -0.046875 to 0.046875
Outputs:
- mixed: float32 [16, 7168], P('groups', ('ctx', 'head')), parts along dimension 0
The draws below stay inside these ranges and needn't reach their ends.
There are 2 independent parts, one for each index of `groups`. The reference program is written for one: setup_inputs(seed, part) draws one part's arguments, and reference() takes and returns one part's arrays. A program takes and returns all parts, laid end to end along the dimension named above; an argument that names none is the same for every part. Nothing has to cross between parts.
Inputs may be any that keep to these rules, and one draw needn't show every extreme that they name: lengths[s] counts the cached positions of sequence s including its 2 new tokens; the largest equals 2048 in every draw.
All inputs are finite; a program needn't handle non-finite values.
Results may differ from the reference program's by a relative error of at most 0.0055.
Values may be sent and summed in bfloat16 or wider, within the bound.
No kernel may reach another device: no remote copies, remote signals or barrier semaphores. Data moves between devices by JAX's collectives and lax.ppermute only.
A program may use at most 64 MiB of HBM per device.

```python
import math
import jax
import jax.numpy as jnp
from jax import lax

D = 7168
H = 128
LATENT_CHANNELS = 512
ROTARY_CHANNELS = 64
PLAIN_CHANNELS = 128
VDIM = 128
DRAFT = 2
SEQS = 4
CTX_DEV = 512
CTX = 2048
ROWS = 8
N_CTX = 4


def pick_longest(key):
    return jax.random.randint(jax.random.fold_in(key, 22), (), 0, SEQS)


def draw_joint(key):
    base_draw = jax.random.normal(jax.random.fold_in(key, 11), (SEQS, CTX, LATENT_CHANNELS + ROTARY_CHANNELS), jnp.float32)
    longest = pick_longest(key)
    offset = jax.random.randint(jax.random.fold_in(key, 23), (), 0, SEQS - 1)
    smallest = (longest + 1 + offset) % SEQS
    seq_iota = jnp.arange(SEQS)
    seq_scale = jnp.exp(jax.random.uniform(jax.random.fold_in(key, 24), (SEQS,), jnp.float32, math.log(0.02), math.log(1.25)))
    seq_scale = jnp.where(seq_iota == longest, jnp.float32(1.25), seq_scale)
    seq_scale = jnp.where(seq_iota == smallest, jnp.float32(0.02), seq_scale)
    run_scale = jnp.exp(jax.random.uniform(jax.random.fold_in(key, 25), (SEQS, 16), jnp.float32, 0.0, math.log(2.0)))
    run_index = jnp.arange(CTX) * 16 // CTX
    key_scale = seq_scale[:, None] * run_scale[:, run_index]
    latent_part = jnp.clip(base_draw[:, :, :LATENT_CHANNELS], -6.0, 6.0)
    rope_part = jnp.clip(base_draw[:, :, LATENT_CHANNELS:] * key_scale[:, :, None], -8.0, 8.0)
    head_order = jax.random.permutation(jax.random.fold_in(key, 26), H)
    sharp = head_order < max(H // 4, 1)
    head_scale = jnp.where(sharp, jnp.float32(60.0), jnp.float32(1.0))
    rope_base = jax.random.normal(jax.random.fold_in(key, 12), (SEQS * DRAFT, H, ROTARY_CHANNELS), jnp.float32)
    rope_draw = jnp.clip(rope_base * head_scale[None, :, None], -500.0, 500.0)
    cache_draw = jnp.concatenate([latent_part, rope_part], axis=2)
    return (cache_draw, rope_draw)


def draw_kv_cache(key, part):
    return draw_joint(key)[0].astype(jnp.bfloat16)


def draw_query_rope(key, part):
    return draw_joint(key)[1].astype(jnp.bfloat16)


def draw_lengths(key, part):
    base_length = jax.random.randint(jax.random.fold_in(key, 21), (SEQS,), DRAFT, CTX + 1)
    longest = pick_longest(key)
    return jnp.where(jnp.arange(SEQS) == longest, CTX, base_length).astype(jnp.int32)


def block_scale(own_key, dims, pieces, least, high):
    def one(dim, blocks):
        steps = jax.random.uniform(jax.random.fold_in(jax.random.fold_in(own_key, 6), dim), (blocks,), jnp.float32, least / len(pieces), high / len(pieces))
        return jnp.repeat(jnp.exp(steps), dims[dim] // blocks).reshape((-1,) + (1,) * (len(dims) - dim - 1))

    level = one(*pieces[0])
    for cut in pieces[1:]:
        level = level * one(*cut)
    return level


def normal_values(own_key, dims, deviation, reach, shards=(), held_as=jnp.bfloat16):
    result = deviation * jax.random.normal(own_key, dims, jnp.float32)
    if shards:
        result = result * block_scale(own_key, dims, shards, -0.22, 0.18)
    return jnp.clip(result, -reach, reach).astype(held_as)


def setup_inputs(seed: int = 0, part: int = 0) -> dict:
    splits = jax.random.split(jax.random.key(seed), 8)
    own_keys = jax.random.split(jax.random.fold_in(splits[7], part), 8)
    return {
        "query_nope": normal_values(own_keys[0], (ROWS, H, PLAIN_CHANNELS), 1.5, 9.0, ((1, 4),)),
        "query_rope": draw_query_rope(jax.random.fold_in(jax.random.fold_in(splits[7], part), 71), part),
        "kv_cache": draw_kv_cache(jax.random.fold_in(jax.random.fold_in(splits[7], part), 71), part),
        "lengths": draw_lengths(jax.random.fold_in(jax.random.fold_in(splits[7], part), 71), part),
        "w_absorb": normal_values(splits[4], (H, PLAIN_CHANNELS, LATENT_CHANNELS), PLAIN_CHANNELS ** -0.5, 0.5, ((0, 4), (2, 4))),
        "w_value": normal_values(splits[5], (H, LATENT_CHANNELS, VDIM), LATENT_CHANNELS ** -0.5, 0.25, ((0, 4), (1, 4))),
        "w_output": normal_values(splits[6], (H * VDIM, D), (H * VDIM) ** -0.5, 0.046875, ((0, 4), (1, 4))),
    }


def one_sequence(items):
    sequence_query, cache_seq, length = items
    cache_float = cache_seq.astype(jnp.float32).reshape(N_CTX, CTX_DEV, LATENT_CHANNELS + ROTARY_CHANNELS)
    logit_scores = jnp.einsum('wp,zsp->zws', sequence_query.astype(jnp.float32), cache_float) * ((PLAIN_CHANNELS + ROTARY_CHANNELS) ** -0.5)
    position = jnp.arange(N_CTX * CTX_DEV, dtype=jnp.int32).reshape(N_CTX, CTX_DEV)
    draft_index = jnp.arange(DRAFT * H, dtype=jnp.int32) // H
    row_limit = length - DRAFT + draft_index
    is_valid = position[:, None, :] <= row_limit[None, :, None]
    masked = jnp.where(is_valid, logit_scores, jnp.float32(-1e30))
    block_top = jnp.max(masked, axis=2)
    expo_f = jnp.where(is_valid, jnp.exp(masked - block_top[:, :, None]), jnp.float32(0.0))
    block_total = jnp.sum(expo_f, axis=2)
    softmax_weights = expo_f.astype(jnp.bfloat16).astype(jnp.float32)
    block_partial_sum = jnp.einsum('mtz,mzj->mtj', softmax_weights, cache_float[:, :, :LATENT_CHANNELS])
    row_top = jnp.max(block_top, axis=0)
    factor = jnp.exp(block_top - row_top[None, :])
    total = jnp.sum(factor * block_total, axis=0)
    weighted = jnp.sum(factor[:, :, None] * block_partial_sum, axis=0)
    return (weighted / total[:, None]).astype(jnp.bfloat16)


def reference(query_nope, query_rope, kv_cache, lengths, w_absorb, w_value, w_output):
    q_latent = jnp.einsum('rhn,hnl->rhl', query_nope.astype(jnp.float32), w_absorb.astype(jnp.float32)).astype(jnp.bfloat16)
    query_rows = jnp.concatenate([q_latent, query_rope], axis=2).reshape(SEQS, DRAFT * H, LATENT_CHANNELS + ROTARY_CHANNELS)
    latent_out = lax.map(one_sequence, (query_rows, kv_cache, lengths))
    latent_out = latent_out.reshape(SEQS * DRAFT, H, LATENT_CHANNELS)
    values = jnp.einsum('rhl,hlv->rhv', latent_out.astype(jnp.float32), w_value.astype(jnp.float32)).astype(jnp.bfloat16)
    mixed = jnp.dot(values.reshape(SEQS * DRAFT, H * VDIM), w_output, preferred_element_type=jnp.float32)
    return mixed
```

```python
import functools

import jax
import jax.numpy as jnp
from jax import lax
from jax.sharding import PartitionSpec as P

ROTARY_CHANNELS = 64
PLAIN_CHANNELS = 128
DRAFT = 2
PERMUTE_MAX = 8


def shift_pairs(n, k):
    return [(i, (i + k) % n) for i in range(n)]


def gather_pieces(x, axis, n):
    if n > PERMUTE_MAX:
        return lax.all_gather(x, axis, axis=0, tiled=False)
    me = lax.axis_index(axis)
    received = [x] + [lax.ppermute(x, axis, shift_pairs(n, k)) for k in range(1, n)]
    back = jnp.stack([received[(-j) % n] for j in range(n)])
    return jnp.roll(back, me, axis=0)


def exchange_sum(chunks, axis, n, combine):
    if n > PERMUTE_MAX:
        got = lax.all_to_all(chunks, axis, 0, 0, tiled=False)
        return combine([got[j] for j in range(n)])
    me = lax.axis_index(axis)
    mine = [lax.dynamic_index_in_dim(chunks, me, axis=0, keepdims=False)]
    for k in range(1, n):
        out = lax.dynamic_index_in_dim(chunks, (me + k) % n, axis=0, keepdims=False)
        mine.append(lax.ppermute(out, axis, shift_pairs(n, k)))
    return combine(mine)


def per_device(n_ctx, n_head, query_nope, query_rope, kv_cache, lengths, w_absorb, w_value, w_output):
    seq_count, ctx_rows, channels = kv_cache.shape
    row_count, head_count = query_nope.shape[:2]
    latent_width = channels - query_rope.shape[2]
    slice_width = w_value.shape[1]

    q_part = jnp.einsum(
        "rhn,hnl->rhl", query_nope, w_absorb, preferred_element_type=jnp.float32
    ).astype(jnp.bfloat16)
    q_pieces = gather_pieces(q_part, "ctx", n_ctx)
    q_latent = jnp.concatenate([q_pieces[j] for j in range(n_ctx)], axis=2)
    query_rows = jnp.concatenate([q_latent, query_rope], axis=2).reshape(
        seq_count, DRAFT * head_count, channels
    )
    logit_scores = jnp.einsum(
        "sqc,skc->sqk", query_rows, kv_cache, preferred_element_type=jnp.float32
    ) * (PLAIN_CHANNELS + ROTARY_CHANNELS) ** (-0.5)
    position = lax.axis_index("ctx") * ctx_rows + jnp.arange(ctx_rows, dtype=jnp.int32)
    draft_index = jnp.arange(DRAFT * head_count, dtype=jnp.int32) // head_count
    row_limit = lengths[:, None] - DRAFT + draft_index[None, :]
    is_valid = position[None, None, :] <= row_limit[:, :, None]
    masked = jnp.where(is_valid, logit_scores, jnp.float32(-1e30))
    block_top = jnp.max(masked, axis=2)
    expo_f = jnp.where(is_valid, jnp.exp(masked - block_top[:, :, None]), jnp.float32(0.0))
    block_total = jnp.sum(expo_f, axis=2)
    weighted = jnp.einsum(
        "sqk,skl->sql",
        expo_f.astype(jnp.bfloat16),
        kv_cache[:, :, :latent_width],
        preferred_element_type=jnp.float32,
    )
    sums = jnp.moveaxis(weighted.reshape(seq_count, DRAFT * head_count, n_ctx, slice_width), 2, 0)
    stats = jnp.broadcast_to(
        jnp.stack([block_top, block_total])[None], (n_ctx, 2) + block_top.shape
    )

    def combine_blocks(parts):
        tops = [st[0] for _, st in parts]
        row_top = functools.reduce(jnp.maximum, tops)
        factors = [jnp.exp(t - row_top) for t in tops]
        total = sum(f * st[1] for f, (_, st) in zip(factors, parts))
        acc = sum(f[:, :, None] * s for f, (s, _) in zip(factors, parts))
        return (acc / total[:, :, None]).astype(jnp.bfloat16)

    if n_ctx > PERMUTE_MAX:
        got_s = lax.all_to_all(sums, "ctx", 0, 0, tiled=False)
        got_t = lax.all_to_all(stats, "ctx", 0, 0, tiled=False)
        latent_out = combine_blocks([(got_s[j], got_t[j]) for j in range(n_ctx)])
    else:
        me = lax.axis_index("ctx")
        parts = [(
            lax.dynamic_index_in_dim(sums, me, axis=0, keepdims=False),
            jnp.stack([block_top, block_total]),
        )]
        for k in range(1, n_ctx):
            out = lax.dynamic_index_in_dim(sums, (me + k) % n_ctx, axis=0, keepdims=False)
            parts.append((
                lax.ppermute(out, "ctx", shift_pairs(n_ctx, k)),
                lax.ppermute(jnp.stack([block_top, block_total]), "ctx", shift_pairs(n_ctx, k)),
            ))
        latent_out = combine_blocks(parts)

    latent_out = latent_out.reshape(row_count, head_count, slice_width)
    value_part = jnp.einsum("rhl,hlv->rhv", latent_out, w_value, preferred_element_type=jnp.float32)
    if n_ctx > PERMUTE_MAX:
        values = lax.psum(value_part, "ctx").astype(jnp.bfloat16)
    else:
        received = [value_part] + [
            lax.ppermute(value_part, "ctx", shift_pairs(n_ctx, k)) for k in range(1, n_ctx)
        ]
        values = sum(received).astype(jnp.bfloat16)
    partial_value = jnp.dot(
        values.reshape(row_count, -1), w_output, preferred_element_type=jnp.float32
    )
    if n_head > PERMUTE_MAX:
        return lax.psum_scatter(partial_value, "head", scatter_dimension=1, tiled=True)
    out_width = partial_value.shape[1] // n_head
    chunks = jnp.moveaxis(partial_value.reshape(row_count, n_head, out_width), 1, 0)
    return exchange_sum(chunks, "head", n_head, sum)


def solution(mesh):
    return jax.shard_map(
        functools.partial(per_device, mesh.shape["ctx"], mesh.shape["head"]),
        mesh=mesh,
        in_specs=(
            P("groups", "head", None),
            P("groups", "head", None),
            P("groups", "ctx", None),
            P("groups"),
            P("head", None, "ctx"),
            P("head", "ctx", None),
            P("head", "ctx"),
        ),
        out_specs=P("groups", ("ctx", "head")),
        check_vma=False,
    )
```

```python
import functools

import jax
import jax.numpy as jnp
from jax import lax
from jax.sharding import PartitionSpec as P

ROTARY_CHANNELS = 64
PLAIN_CHANNELS = 128
DRAFT = 2
PERMUTE_MAX = 8


def shift_pairs(n, k):
    return [(i, (i + k) % n) for i in range(n)]


def pick(index, options):
    chosen = options[-1]
    for j in range(len(options) - 2, -1, -1):
        chosen = jnp.where(index == j, options[j], chosen)
    return chosen


def per_device(n_ctx, n_head, query_nope, query_rope, kv_cache, lengths, w_absorb, w_value, w_output):
    seq_count, ctx_rows, channels = kv_cache.shape
    row_count, head_count = query_nope.shape[:2]
    latent_width = channels - query_rope.shape[2]
    slice_width = w_value.shape[1]
    small_ctx = n_ctx <= PERMUTE_MAX
    me_ctx = lax.axis_index("ctx")

    q_part = jnp.einsum(
        "rhn,hnl->rhl", query_nope, w_absorb, preferred_element_type=jnp.float32
    ).astype(jnp.bfloat16)
    if small_ctx:
        received = [q_part] + [
            lax.ppermute(q_part, "ctx", shift_pairs(n_ctx, k)) for k in range(1, n_ctx)
        ]
        slots = [pick((me_ctx - j) % n_ctx, received) for j in range(n_ctx)]
        q_latent = jnp.concatenate(slots, axis=2)
    else:
        q_latent = lax.all_gather(q_part, "ctx", axis=2, tiled=True)
    query_rows = jnp.concatenate([q_latent, query_rope], axis=2).reshape(
        seq_count, DRAFT * head_count, channels
    )
    logit_scores = jnp.einsum(
        "sqc,skc->sqk", query_rows, kv_cache, preferred_element_type=jnp.float32
    ) * (PLAIN_CHANNELS + ROTARY_CHANNELS) ** (-0.5)
    position = me_ctx * ctx_rows + jnp.arange(ctx_rows, dtype=jnp.int32)
    draft_index = jnp.arange(DRAFT * head_count, dtype=jnp.int32) // head_count
    row_limit = lengths[:, None] - DRAFT + draft_index[None, :]
    is_valid = position[None, None, :] <= row_limit[:, :, None]
    masked = jnp.where(is_valid, logit_scores, jnp.float32(-1e30))
    block_top = jnp.max(masked, axis=2)
    expo_f = jnp.where(is_valid, jnp.exp(masked - block_top[:, :, None]), jnp.float32(0.0))
    block_total = jnp.sum(expo_f, axis=2)
    weighted = jnp.einsum(
        "sqk,skl->sql",
        expo_f.astype(jnp.bfloat16),
        kv_cache[:, :, :latent_width],
        preferred_element_type=jnp.float32,
    )
    q_rows = DRAFT * head_count
    stats = jnp.stack([block_top, block_total]).reshape(-1, slice_width)
    sum_slices = [
        weighted[:, :, j * slice_width:(j + 1) * slice_width].reshape(-1, slice_width)
        for j in range(n_ctx)
    ]

    def packed_for(target):
        return jnp.concatenate([pick(target, sum_slices), stats], axis=0)

    def combine_blocks(parts):
        split = seq_count * q_rows
        sums = [p[:split].reshape(seq_count, q_rows, slice_width) for p in parts]
        st = [p[split:].reshape(2, seq_count, q_rows) for p in parts]
        row_top = functools.reduce(jnp.maximum, [t[0] for t in st])
        factors = [jnp.exp(t[0] - row_top) for t in st]
        total = sum(f * t[1] for f, t in zip(factors, st))
        acc = sum(f[:, :, None] * a for f, a in zip(factors, sums))
        return (acc / total[:, :, None]).astype(jnp.bfloat16)

    if small_ctx:
        parts = [packed_for(me_ctx)] + [
            lax.ppermute(packed_for((me_ctx + k) % n_ctx), "ctx", shift_pairs(n_ctx, k))
            for k in range(1, n_ctx)
        ]
    else:
        packed = jnp.stack([jnp.concatenate([s, stats], axis=0) for s in sum_slices])
        got = lax.all_to_all(packed, "ctx", 0, 0, tiled=False)
        parts = [got[j] for j in range(n_ctx)]
    latent_out = combine_blocks(parts).reshape(row_count, head_count, slice_width)

    value_part = jnp.einsum("rhl,hlv->rhv", latent_out, w_value, preferred_element_type=jnp.float32)
    if small_ctx:
        received = [value_part] + [
            lax.ppermute(value_part, "ctx", shift_pairs(n_ctx, k)) for k in range(1, n_ctx)
        ]
        values = sum(received).astype(jnp.bfloat16)
    else:
        values = lax.psum(value_part, "ctx").astype(jnp.bfloat16)
    partial_value = jnp.dot(
        values.reshape(row_count, -1), w_output, preferred_element_type=jnp.float32
    )
    if n_head > PERMUTE_MAX:
        return lax.psum_scatter(partial_value, "head", scatter_dimension=1, tiled=True)
    me_head = lax.axis_index("head")
    out_width = partial_value.shape[1] // n_head
    col_slices = [partial_value[:, j * out_width:(j + 1) * out_width] for j in range(n_head)]
    total = pick(me_head, col_slices)
    for k in range(1, n_head):
        total = total + lax.ppermute(
            pick((me_head + k) % n_head, col_slices), "head", shift_pairs(n_head, k)
        )
    return total


def solution(mesh):
    return jax.shard_map(
        functools.partial(per_device, mesh.shape["ctx"], mesh.shape["head"]),
        mesh=mesh,
        in_specs=(
            P("groups", "head", None),
            P("groups", "head", None),
            P("groups", "ctx", None),
            P("groups"),
            P("head", None, "ctx"),
            P("head", "ctx", None),
            P("head", "ctx"),
        ),
        out_specs=P("groups", ("ctx", "head")),
        check_vma=False,
    )
```

```python
import functools

import jax
import jax.numpy as jnp
from jax import lax
from jax.experimental import pallas as pl
from jax.experimental.pallas import tpu as pltpu
from jax.sharding import PartitionSpec as P

ROTARY_CHANNELS = 64
PLAIN_CHANNELS = 128
DRAFT = 2
PERMUTE_MAX = 8


def shift_pairs(n, k):
    return [(i, (i + k) % n) for i in range(n)]


def pick(index, options):
    chosen = options[-1]
    for j in range(len(options) - 2, -1, -1):
        chosen = jnp.where(index == j, options[j], chosen)
    return chosen


def out_proj_kernel(chunks, v_ref, w_hbm, o_ref, w_vmem, sems):
    depth = w_hbm.shape[0] // chunks
    copies = [
        pltpu.make_async_copy(
            w_hbm.at[pl.ds(i * depth, depth)], w_vmem.at[pl.ds(i * depth, depth)], sems.at[i]
        )
        for i in range(chunks)
    ]
    for c in copies:
        c.start()
    acc = jnp.zeros(o_ref.shape, jnp.float32)
    for i in range(chunks):
        copies[i].wait()
        rows = pl.ds(i * depth, depth)
        acc = acc + jnp.dot(v_ref[:, rows], w_vmem[rows, :], preferred_element_type=jnp.float32)
    o_ref[...] = acc


def out_proj(values, w_output):
    depth, width = w_output.shape
    chunks = 8 if depth % (8 * 256) == 0 else 1
    vmem = pltpu.MemorySpace.VMEM
    return pl.pallas_call(
        functools.partial(out_proj_kernel, chunks),
        out_shape=jax.ShapeDtypeStruct((values.shape[0], width), jnp.float32),
        in_specs=[pl.BlockSpec(memory_space=vmem), pl.BlockSpec(memory_space=pl.ANY)],
        out_specs=pl.BlockSpec(memory_space=vmem),
        scratch_shapes=[
            pltpu.VMEM(w_output.shape, w_output.dtype),
            pltpu.SemaphoreType.DMA((chunks,)),
        ],
        cost_estimate=pl.CostEstimate(
            flops=2 * values.shape[0] * depth * width,
            transcendentals=0,
            bytes_accessed=2 * depth * width + 2 * values.size + 4 * values.shape[0] * width,
        ),
    )(values, w_output)


def per_device(n_ctx, n_head, query_nope, query_rope, kv_cache, lengths, w_absorb, w_value, w_output):
    seq_count, ctx_rows, channels = kv_cache.shape
    row_count, head_count = query_nope.shape[:2]
    latent_width = channels - query_rope.shape[2]
    slice_width = w_value.shape[1]
    small_ctx = n_ctx <= PERMUTE_MAX
    me_ctx = lax.axis_index("ctx")

    q_part = jnp.einsum(
        "rhn,hnl->rhl", query_nope, w_absorb, preferred_element_type=jnp.float32
    ).astype(jnp.bfloat16)
    if small_ctx:
        received = [q_part] + [
            lax.ppermute(q_part, "ctx", shift_pairs(n_ctx, k)) for k in range(1, n_ctx)
        ]
        slots = [pick((me_ctx - j) % n_ctx, received) for j in range(n_ctx)]
        q_latent = jnp.concatenate(slots, axis=2)
    else:
        q_latent = lax.all_gather(q_part, "ctx", axis=2, tiled=True)
    query_rows = jnp.concatenate([q_latent, query_rope], axis=2).reshape(
        seq_count, DRAFT * head_count, channels
    )
    logit_scores = jnp.einsum(
        "sqc,skc->sqk", query_rows, kv_cache, preferred_element_type=jnp.float32
    ) * (PLAIN_CHANNELS + ROTARY_CHANNELS) ** (-0.5)
    position = me_ctx * ctx_rows + jnp.arange(ctx_rows, dtype=jnp.int32)
    draft_index = jnp.arange(DRAFT * head_count, dtype=jnp.int32) // head_count
    row_limit = lengths[:, None] - DRAFT + draft_index[None, :]
    is_valid = position[None, None, :] <= row_limit[:, :, None]
    masked = jnp.where(is_valid, logit_scores, jnp.float32(-1e30))
    block_top = jnp.max(masked, axis=2)
    expo_f = jnp.where(is_valid, jnp.exp(masked - block_top[:, :, None]), jnp.float32(0.0))
    block_total = jnp.sum(expo_f, axis=2)
    weighted = jnp.einsum(
        "sqk,skl->sql",
        expo_f.astype(jnp.bfloat16),
        kv_cache[:, :, :latent_width],
        preferred_element_type=jnp.float32,
    )
    q_rows = DRAFT * head_count
    stats = jnp.stack([block_top, block_total]).reshape(-1, slice_width)
    sum_slices = [
        weighted[:, :, j * slice_width:(j + 1) * slice_width].reshape(-1, slice_width)
        for j in range(n_ctx)
    ]

    def packed_for(target):
        return jnp.concatenate([pick(target, sum_slices), stats], axis=0)

    def combine_blocks(parts):
        split = seq_count * q_rows
        sums = [p[:split].reshape(seq_count, q_rows, slice_width) for p in parts]
        st = [p[split:].reshape(2, seq_count, q_rows) for p in parts]
        row_top = functools.reduce(jnp.maximum, [t[0] for t in st])
        factors = [jnp.exp(t[0] - row_top) for t in st]
        total = sum(f * t[1] for f, t in zip(factors, st))
        acc = sum(f[:, :, None] * a for f, a in zip(factors, sums))
        return (acc / total[:, :, None]).astype(jnp.bfloat16)

    if small_ctx:
        parts = [packed_for(me_ctx)] + [
            lax.ppermute(packed_for((me_ctx + k) % n_ctx), "ctx", shift_pairs(n_ctx, k))
            for k in range(1, n_ctx)
        ]
    else:
        packed = jnp.stack([jnp.concatenate([s, stats], axis=0) for s in sum_slices])
        got = lax.all_to_all(packed, "ctx", 0, 0, tiled=False)
        parts = [got[j] for j in range(n_ctx)]
    latent_out = combine_blocks(parts).reshape(row_count, head_count, slice_width)

    value_part = jnp.einsum("rhl,hlv->rhv", latent_out, w_value, preferred_element_type=jnp.float32)
    if small_ctx:
        received = [value_part] + [
            lax.ppermute(value_part, "ctx", shift_pairs(n_ctx, k)) for k in range(1, n_ctx)
        ]
        values = sum(received).astype(jnp.bfloat16)
    else:
        values = lax.psum(value_part, "ctx").astype(jnp.bfloat16)
    partial_value = out_proj(values.reshape(row_count, -1), w_output)
    if n_head > PERMUTE_MAX:
        return lax.psum_scatter(partial_value, "head", scatter_dimension=1, tiled=True)
    me_head = lax.axis_index("head")
    out_width = partial_value.shape[1] // n_head
    col_slices = [partial_value[:, j * out_width:(j + 1) * out_width] for j in range(n_head)]
    total = pick(me_head, col_slices)
    for k in range(1, n_head):
        total = total + lax.ppermute(
            pick((me_head + k) % n_head, col_slices), "head", shift_pairs(n_head, k)
        )
    return total


def solution(mesh):
    return jax.shard_map(
        functools.partial(per_device, mesh.shape["ctx"], mesh.shape["head"]),
        mesh=mesh,
        in_specs=(
            P("groups", "head", None),
            P("groups", "head", None),
            P("groups", "ctx", None),
            P("groups"),
            P("head", None, "ctx"),
            P("head", "ctx", None),
            P("head", "ctx"),
        ),
        out_specs=P("groups", ("ctx", "head")),
        check_vma=False,
    )
```

```python
import functools

import jax
import jax.numpy as jnp
from jax import lax
from jax.sharding import PartitionSpec as P

ROTARY_CHANNELS = 64
PLAIN_CHANNELS = 128
DRAFT = 2
PERMUTE_MAX = 8


def shift_pairs(n, k):
    return [(i, (i + k) % n) for i in range(n)]


def pick(index, options):
    chosen = options[-1]
    for j in range(len(options) - 2, -1, -1):
        chosen = jnp.where(index == j, options[j], chosen)
    return chosen


def per_device(n_ctx, n_head, query_nope, query_rope, kv_cache, lengths, w_absorb, w_value, w_output):
    seq_count, ctx_rows, channels = kv_cache.shape
    row_count, head_count = query_nope.shape[:2]
    latent_width = channels - query_rope.shape[2]
    slice_width = w_value.shape[1]
    small_ctx = n_ctx <= PERMUTE_MAX
    me_ctx = lax.axis_index("ctx")

    q_part = jnp.einsum(
        "rhn,hnl->rhl", query_nope, w_absorb, preferred_element_type=jnp.float32
    ).astype(jnp.bfloat16)
    if small_ctx:
        received = [q_part] + [
            lax.ppermute(q_part, "ctx", shift_pairs(n_ctx, k)) for k in range(1, n_ctx)
        ]
        source = (me_ctx - jnp.arange(n_ctx, dtype=jnp.int32)[None, None, :, None]) % n_ctx
        q_slots = received[-1][:, :, None, :]
        for k in range(n_ctx - 2, -1, -1):
            q_slots = jnp.where(source == k, received[k][:, :, None, :], q_slots)
        q_latent = q_slots.reshape(row_count, head_count, latent_width)
    else:
        q_latent = lax.all_gather(q_part, "ctx", axis=2, tiled=True)
    q_rows = DRAFT * head_count
    latent_scores = jnp.einsum(
        "sqc,skc->sqk",
        q_latent.reshape(seq_count, q_rows, latent_width),
        kv_cache[:, :, :latent_width],
        preferred_element_type=jnp.float32,
    )
    rope_scores = jnp.einsum(
        "sqc,skc->sqk",
        query_rope.reshape(seq_count, q_rows, channels - latent_width),
        kv_cache[:, :, latent_width:],
        preferred_element_type=jnp.float32,
    )
    logit_scores = (latent_scores + rope_scores) * (PLAIN_CHANNELS + ROTARY_CHANNELS) ** (-0.5)
    position = me_ctx * ctx_rows + jnp.arange(ctx_rows, dtype=jnp.int32)
    draft_index = jnp.arange(DRAFT * head_count, dtype=jnp.int32) // head_count
    row_limit = lengths[:, None] - DRAFT + draft_index[None, :]
    is_valid = position[None, None, :] <= row_limit[:, :, None]
    masked = jnp.where(is_valid, logit_scores, jnp.float32(-1e30))
    block_top = jnp.max(masked, axis=2)
    expo_f = jnp.where(is_valid, jnp.exp(masked - block_top[:, :, None]), jnp.float32(0.0))
    block_total = jnp.sum(expo_f, axis=2)
    weighted = jnp.einsum(
        "sqk,skl->sql",
        expo_f.astype(jnp.bfloat16),
        kv_cache[:, :, :latent_width],
        preferred_element_type=jnp.float32,
    )
    stats = jnp.stack([block_top, block_total]).reshape(-1, slice_width)
    sum_slices = [
        weighted[:, :, j * slice_width:(j + 1) * slice_width].reshape(-1, slice_width)
        for j in range(n_ctx)
    ]

    def packed_for(target):
        return jnp.concatenate([pick(target, sum_slices), stats], axis=0)

    def combine_blocks(parts):
        split = seq_count * q_rows
        sums = [p[:split].reshape(seq_count, q_rows, slice_width) for p in parts]
        st = [p[split:].reshape(2, seq_count, q_rows) for p in parts]
        row_top = functools.reduce(jnp.maximum, [t[0] for t in st])
        factors = [jnp.exp(t[0] - row_top) for t in st]
        total = sum(f * t[1] for f, t in zip(factors, st))
        acc = sum(f[:, :, None] * a for f, a in zip(factors, sums))
        return (acc / total[:, :, None]).astype(jnp.bfloat16)

    if small_ctx:
        parts = [packed_for(me_ctx)] + [
            lax.ppermute(packed_for((me_ctx + k) % n_ctx), "ctx", shift_pairs(n_ctx, k))
            for k in range(1, n_ctx)
        ]
    else:
        packed = jnp.stack([jnp.concatenate([s, stats], axis=0) for s in sum_slices])
        got = lax.all_to_all(packed, "ctx", 0, 0, tiled=False)
        parts = [got[j] for j in range(n_ctx)]
    latent_out = combine_blocks(parts).reshape(row_count, head_count, slice_width)

    value_part = jnp.einsum("rhl,hlv->rhv", latent_out, w_value, preferred_element_type=jnp.float32)
    if small_ctx:
        received = [value_part] + [
            lax.ppermute(value_part, "ctx", shift_pairs(n_ctx, k)) for k in range(1, n_ctx)
        ]
        values = sum(received).astype(jnp.bfloat16)
    else:
        values = lax.psum(value_part, "ctx").astype(jnp.bfloat16)
    partial_value = jnp.dot(
        values.reshape(row_count, -1), w_output, preferred_element_type=jnp.float32
    )
    if n_head > PERMUTE_MAX:
        return lax.psum_scatter(partial_value, "head", scatter_dimension=1, tiled=True)
    me_head = lax.axis_index("head")
    out_width = partial_value.shape[1] // n_head
    col_slices = [partial_value[:, j * out_width:(j + 1) * out_width] for j in range(n_head)]
    total = pick(me_head, col_slices)
    for k in range(1, n_head):
        total = total + lax.ppermute(
            pick((me_head + k) % n_head, col_slices), "head", shift_pairs(n_head, k)
        )
    return total


def solution(mesh):
    return jax.shard_map(
        functools.partial(per_device, mesh.shape["ctx"], mesh.shape["head"]),
        mesh=mesh,
        in_specs=(
            P("groups", "head", None),
            P("groups", "head", None),
            P("groups", "ctx", None),
            P("groups"),
            P("head", None, "ctx"),
            P("head", "ctx", None),
            P("head", "ctx"),
        ),
        out_specs=P("groups", ("ctx", "head")),
        check_vma=False,
    )
```

```python
import functools

import jax
import jax.numpy as jnp
from jax import lax
from jax.sharding import PartitionSpec as P

ROTARY_CHANNELS = 64
PLAIN_CHANNELS = 128
DRAFT = 2
PERMUTE_MAX = 8


def shift_pairs(n, k):
    return [(i, (i + k) % n) for i in range(n)]


def pick(index, options):
    chosen = options[-1]
    for j in range(len(options) - 2, -1, -1):
        chosen = jnp.where(index == j, options[j], chosen)
    return chosen


def per_device(n_ctx, n_head, query_nope, query_rope, kv_cache, lengths, w_absorb, w_value, w_output):
    seq_count, ctx_rows, channels = kv_cache.shape
    row_count, head_count = query_nope.shape[:2]
    latent_width = channels - query_rope.shape[2]
    slice_width = w_value.shape[1]
    small_ctx = n_ctx <= PERMUTE_MAX
    me_ctx = lax.axis_index("ctx")

    q_part = jnp.einsum(
        "rhn,hnl->rhl", query_nope, w_absorb, preferred_element_type=jnp.float32
    ).astype(jnp.bfloat16)
    if small_ctx:
        received = [q_part] + [
            lax.ppermute(q_part, "ctx", shift_pairs(n_ctx, k)) for k in range(1, n_ctx)
        ]
        source = (me_ctx - jnp.arange(n_ctx, dtype=jnp.int32)[None, None, :, None]) % n_ctx
        q_slots = received[-1][:, :, None, :]
        for k in range(n_ctx - 2, -1, -1):
            q_slots = jnp.where(source == k, received[k][:, :, None, :], q_slots)
        q_latent = q_slots.reshape(row_count, head_count, latent_width)
    else:
        q_latent = lax.all_gather(q_part, "ctx", axis=2, tiled=True)
    q_rows = DRAFT * head_count
    latent_scores = jnp.einsum(
        "sqc,skc->sqk",
        q_latent.reshape(seq_count, q_rows, latent_width),
        kv_cache[:, :, :latent_width],
        preferred_element_type=jnp.float32,
    )
    rope_scores = jnp.einsum(
        "sqc,skc->sqk",
        query_rope.reshape(seq_count, q_rows, channels - latent_width),
        kv_cache[:, :, latent_width:],
        preferred_element_type=jnp.float32,
    )
    logit_scores = (latent_scores + rope_scores) * (PLAIN_CHANNELS + ROTARY_CHANNELS) ** (-0.5)
    position = me_ctx * ctx_rows + jnp.arange(ctx_rows, dtype=jnp.int32)
    draft_index = jnp.arange(DRAFT * head_count, dtype=jnp.int32) // head_count
    row_limit = lengths[:, None] - DRAFT + draft_index[None, :]
    is_valid = position[None, None, :] <= row_limit[:, :, None]
    masked = jnp.where(is_valid, logit_scores, jnp.float32(-1e30))
    block_top = jnp.max(masked, axis=2)
    expo_f = jnp.where(is_valid, jnp.exp(masked - block_top[:, :, None]), jnp.float32(0.0))
    block_total = jnp.sum(expo_f, axis=2)
    weighted = jnp.einsum(
        "sqk,skl->sql",
        expo_f.astype(jnp.bfloat16),
        kv_cache[:, :, :latent_width],
        preferred_element_type=jnp.float32,
    )
    stats = jnp.stack([block_top, block_total]).reshape(-1, slice_width)
    sum_slices = [
        weighted[:, :, j * slice_width:(j + 1) * slice_width].reshape(-1, slice_width)
        for j in range(n_ctx)
    ]

    def to_bf16_grid(x):
        return lax.reduce_precision(x, exponent_bits=8, mantissa_bits=7)

    hi = to_bf16_grid(stats)
    mid = to_bf16_grid(stats - hi)
    stats_hi = hi.astype(jnp.bfloat16)
    stats_mid = mid.astype(jnp.bfloat16)
    stats_lo = ((stats - hi) - mid).astype(jnp.bfloat16)
    stat_rows = stats.shape[0]

    def packed_for(target):
        return jnp.concatenate(
            [pick(target, sum_slices).astype(jnp.bfloat16), stats_hi, stats_mid, stats_lo], axis=0
        )

    def unpack(p):
        split = seq_count * q_rows
        f = p[split:].astype(jnp.float32)
        whole = (f[:stat_rows] + f[stat_rows:2 * stat_rows]) + f[2 * stat_rows:]
        return p[:split].astype(jnp.float32), whole

    def combine_blocks(parts):
        sums = [a.reshape(seq_count, q_rows, slice_width) for a, _ in parts]
        st = [b.reshape(2, seq_count, q_rows) for _, b in parts]
        row_top = functools.reduce(jnp.maximum, [t[0] for t in st])
        factors = [jnp.exp(t[0] - row_top) for t in st]
        total = sum(f * t[1] for f, t in zip(factors, st))
        acc = sum(f[:, :, None] * a for f, a in zip(factors, sums))
        return (acc / total[:, :, None]).astype(jnp.bfloat16)

    if small_ctx:
        parts = [(pick(me_ctx, sum_slices), stats)] + [
            unpack(lax.ppermute(packed_for((me_ctx + k) % n_ctx), "ctx", shift_pairs(n_ctx, k)))
            for k in range(1, n_ctx)
        ]
    else:
        packed = jnp.stack([jnp.concatenate([s, stats], axis=0) for s in sum_slices])
        got = lax.all_to_all(packed, "ctx", 0, 0, tiled=False)
        split = seq_count * q_rows
        parts = [(got[j][:split], got[j][split:]) for j in range(n_ctx)]
    latent_out = combine_blocks(parts).reshape(row_count, head_count, slice_width)

    value_part = jnp.einsum("rhl,hlv->rhv", latent_out, w_value, preferred_element_type=jnp.float32)
    if small_ctx:
        sent = value_part.astype(jnp.bfloat16)
        received = [value_part] + [
            lax.ppermute(sent, "ctx", shift_pairs(n_ctx, k)).astype(jnp.float32)
            for k in range(1, n_ctx)
        ]
        values = sum(received).astype(jnp.bfloat16)
    else:
        values = lax.psum(value_part, "ctx").astype(jnp.bfloat16)
    partial_value = jnp.dot(
        values.reshape(row_count, -1), w_output, preferred_element_type=jnp.float32
    )
    if n_head > PERMUTE_MAX:
        return lax.psum_scatter(partial_value, "head", scatter_dimension=1, tiled=True)
    me_head = lax.axis_index("head")
    out_width = partial_value.shape[1] // n_head
    col_slices = [partial_value[:, j * out_width:(j + 1) * out_width] for j in range(n_head)]
    total = pick(me_head, col_slices)
    for k in range(1, n_head):
        total = total + lax.ppermute(
            pick((me_head + k) % n_head, col_slices), "head", shift_pairs(n_head, k)
        )
    return total


def solution(mesh):
    return jax.shard_map(
        functools.partial(per_device, mesh.shape["ctx"], mesh.shape["head"]),
        mesh=mesh,
        in_specs=(
            P("groups", "head", None),
            P("groups", "head", None),
            P("groups", "ctx", None),
            P("groups"),
            P("head", None, "ctx"),
            P("head", "ctx", None),
            P("head", "ctx"),
        ),
        out_specs=P("groups", ("ctx", "head")),
        check_vma=False,
    )
```

```python
import functools

import jax
import jax.numpy as jnp
from jax import lax
from jax.sharding import PartitionSpec as P

ROTARY_CHANNELS = 64
PLAIN_CHANNELS = 128
DRAFT = 2
PERMUTE_MAX = 8


def shift_pairs(n, k):
    return [(i, (i + k) % n) for i in range(n)]


def pick(index, options):
    chosen = options[-1]
    for j in range(len(options) - 2, -1, -1):
        chosen = jnp.where(index == j, options[j], chosen)
    return chosen


def per_device(n_ctx, n_head, query_nope, query_rope, kv_cache, lengths, w_absorb, w_value, w_output):
    seq_count, ctx_rows, channels = kv_cache.shape
    row_count, head_count = query_nope.shape[:2]
    latent_width = channels - query_rope.shape[2]
    slice_width = w_value.shape[1]
    small_ctx = n_ctx <= PERMUTE_MAX
    me_ctx = lax.axis_index("ctx")

    q_part = jnp.einsum(
        "rhn,hnl->rhl", query_nope, w_absorb, preferred_element_type=jnp.float32
    ).astype(jnp.bfloat16)
    if small_ctx:
        received = [q_part] + [
            lax.ppermute(q_part, "ctx", shift_pairs(n_ctx, k)) for k in range(1, n_ctx)
        ]
        source = (me_ctx - jnp.arange(n_ctx, dtype=jnp.int32)[None, None, :, None]) % n_ctx
        q_slots = received[-1][:, :, None, :]
        for k in range(n_ctx - 2, -1, -1):
            q_slots = jnp.where(source == k, received[k][:, :, None, :], q_slots)
        q_latent = q_slots.reshape(row_count, head_count, latent_width)
    else:
        q_latent = lax.all_gather(q_part, "ctx", axis=2, tiled=True)
    q_rows = DRAFT * head_count
    latent_scores = jnp.einsum(
        "sqc,skc->sqk",
        q_latent.reshape(seq_count, q_rows, latent_width),
        kv_cache[:, :, :latent_width],
        preferred_element_type=jnp.float32,
    )
    rope_scores = jnp.einsum(
        "sqc,skc->sqk",
        query_rope.reshape(seq_count, q_rows, channels - latent_width),
        kv_cache[:, :, latent_width:],
        preferred_element_type=jnp.float32,
    )
    logit_scores = (latent_scores + rope_scores) * (PLAIN_CHANNELS + ROTARY_CHANNELS) ** (-0.5)
    position = me_ctx * ctx_rows + jnp.arange(ctx_rows, dtype=jnp.int32)
    draft_index = jnp.arange(DRAFT * head_count, dtype=jnp.int32) // head_count
    row_limit = lengths[:, None] - DRAFT + draft_index[None, :]
    is_valid = position[None, None, :] <= row_limit[:, :, None]
    masked = jnp.where(is_valid, logit_scores, jnp.float32(-1e30))
    block_top = jnp.max(masked, axis=2)
    expo_f = jnp.where(is_valid, jnp.exp(masked - block_top[:, :, None]), jnp.float32(0.0))
    block_total = jnp.sum(expo_f, axis=2)
    weighted = jnp.einsum(
        "sqk,skl->sql",
        expo_f.astype(jnp.bfloat16),
        kv_cache[:, :, :latent_width],
        preferred_element_type=jnp.float32,
    )
    stats = jnp.stack([block_top, block_total]).reshape(-1, slice_width)
    sum_slices = [
        weighted[:, :, j * slice_width:(j + 1) * slice_width].reshape(-1, slice_width)
        for j in range(n_ctx)
    ]

    def to_bf16_grid(x):
        return lax.reduce_precision(x, exponent_bits=8, mantissa_bits=7)

    hi = to_bf16_grid(stats)
    mid = to_bf16_grid(stats - hi)
    stats_hi = hi.astype(jnp.bfloat16)
    stats_mid = mid.astype(jnp.bfloat16)
    stats_lo = ((stats - hi) - mid).astype(jnp.bfloat16)
    stat_rows = stats.shape[0]

    def packed_for(target):
        return jnp.concatenate(
            [pick(target, sum_slices).astype(jnp.bfloat16), stats_hi, stats_mid, stats_lo], axis=0
        )

    def unpack(p):
        split = seq_count * q_rows
        f = p[split:].astype(jnp.float32)
        whole = (f[:stat_rows] + f[stat_rows:2 * stat_rows]) + f[2 * stat_rows:]
        return p[:split].astype(jnp.float32), whole

    def combine_blocks(parts):
        sums = [a.reshape(seq_count, q_rows, slice_width) for a, _ in parts]
        st = [b.reshape(2, seq_count, q_rows) for _, b in parts]
        row_top = functools.reduce(jnp.maximum, [t[0] for t in st])
        factors = [jnp.exp(t[0] - row_top) for t in st]
        total = sum(f * t[1] for f, t in zip(factors, st))
        acc = sum(f[:, :, None] * a for f, a in zip(factors, sums))
        return (acc / total[:, :, None]).astype(jnp.bfloat16)

    if small_ctx:
        parts = [(pick(me_ctx, sum_slices), stats)] + [
            unpack(lax.ppermute(packed_for((me_ctx + k) % n_ctx), "ctx", shift_pairs(n_ctx, k)))
            for k in range(1, n_ctx)
        ]
    else:
        packed = jnp.stack([jnp.concatenate([s, stats], axis=0) for s in sum_slices])
        got = lax.all_to_all(packed, "ctx", 0, 0, tiled=False)
        split = seq_count * q_rows
        parts = [(got[j][:split], got[j][split:]) for j in range(n_ctx)]
    latent_out = combine_blocks(parts).reshape(row_count, head_count, slice_width)

    value_part = jnp.einsum("rhl,hlv->rhv", latent_out, w_value, preferred_element_type=jnp.float32)
    if small_ctx:
        halves = 2 if head_count % 2 == 0 else 1
        span = head_count // halves
        vdim = value_part.shape[2]
        partial_value = 0
        for i in range(halves):
            own = value_part[:, i * span:(i + 1) * span]
            sent = own.astype(jnp.bfloat16)
            received = [own] + [
                lax.ppermute(sent, "ctx", shift_pairs(n_ctx, k)).astype(jnp.float32)
                for k in range(1, n_ctx)
            ]
            values = sum(received).astype(jnp.bfloat16)
            rows = w_output[i * span * vdim:(i + 1) * span * vdim]
            partial_value = partial_value + jnp.dot(
                values.reshape(row_count, -1), rows, preferred_element_type=jnp.float32
            )
    else:
        values = lax.psum(value_part, "ctx").astype(jnp.bfloat16)
        partial_value = jnp.dot(
            values.reshape(row_count, -1), w_output, preferred_element_type=jnp.float32
        )
    if n_head > PERMUTE_MAX:
        return lax.psum_scatter(partial_value, "head", scatter_dimension=1, tiled=True)
    me_head = lax.axis_index("head")
    out_width = partial_value.shape[1] // n_head
    col_slices = [partial_value[:, j * out_width:(j + 1) * out_width] for j in range(n_head)]
    total = pick(me_head, col_slices)
    for k in range(1, n_head):
        total = total + lax.ppermute(
            pick((me_head + k) % n_head, col_slices), "head", shift_pairs(n_head, k)
        )
    return total


def solution(mesh):
    return jax.shard_map(
        functools.partial(per_device, mesh.shape["ctx"], mesh.shape["head"]),
        mesh=mesh,
        in_specs=(
            P("groups", "head", None),
            P("groups", "head", None),
            P("groups", "ctx", None),
            P("groups"),
            P("head", None, "ctx"),
            P("head", "ctx", None),
            P("head", "ctx"),
        ),
        out_specs=P("groups", ("ctx", "head")),
        check_vma=False,
    )
```

```python
import functools

import jax
import jax.numpy as jnp
from jax import lax
from jax.sharding import PartitionSpec as P

ROTARY_CHANNELS = 64
PLAIN_CHANNELS = 128
DRAFT = 2
PERMUTE_MAX = 8


def shift_pairs(n, k):
    return [(i, (i + k) % n) for i in range(n)]


def pick(index, options):
    chosen = options[-1]
    for j in range(len(options) - 2, -1, -1):
        chosen = jnp.where(index == j, options[j], chosen)
    return chosen


def per_device(n_ctx, n_head, query_nope, query_rope, kv_cache, lengths, w_absorb, w_value, w_output):
    seq_count, ctx_rows, channels = kv_cache.shape
    row_count, head_count = query_nope.shape[:2]
    latent_width = channels - query_rope.shape[2]
    slice_width = w_value.shape[1]
    small_ctx = n_ctx <= PERMUTE_MAX
    me_ctx = lax.axis_index("ctx")

    q_part = jnp.einsum(
        "rhn,hnl->rhl", query_nope, w_absorb, preferred_element_type=jnp.float32
    ).astype(jnp.bfloat16)
    if small_ctx:
        received = [q_part] + [
            lax.ppermute(q_part, "ctx", shift_pairs(n_ctx, k)) for k in range(1, n_ctx)
        ]
        source = (me_ctx - jnp.arange(n_ctx, dtype=jnp.int32)[None, None, :, None]) % n_ctx
        q_slots = received[-1][:, :, None, :]
        for k in range(n_ctx - 2, -1, -1):
            q_slots = jnp.where(source == k, received[k][:, :, None, :], q_slots)
        q_latent = lax.optimization_barrier(q_slots.reshape(row_count, head_count, latent_width))
    else:
        q_latent = lax.all_gather(q_part, "ctx", axis=2, tiled=True)
    q_rows = DRAFT * head_count
    latent_scores = jnp.einsum(
        "sqc,skc->sqk",
        q_latent.reshape(seq_count, q_rows, latent_width),
        kv_cache[:, :, :latent_width],
        preferred_element_type=jnp.float32,
    )
    rope_scores = jnp.einsum(
        "sqc,skc->sqk",
        query_rope.reshape(seq_count, q_rows, channels - latent_width),
        kv_cache[:, :, latent_width:],
        preferred_element_type=jnp.float32,
    )
    logit_scores = (latent_scores + rope_scores) * (PLAIN_CHANNELS + ROTARY_CHANNELS) ** (-0.5)
    position = me_ctx * ctx_rows + jnp.arange(ctx_rows, dtype=jnp.int32)
    draft_index = jnp.arange(DRAFT * head_count, dtype=jnp.int32) // head_count
    row_limit = lengths[:, None] - DRAFT + draft_index[None, :]
    is_valid = position[None, None, :] <= row_limit[:, :, None]
    masked = jnp.where(is_valid, logit_scores, jnp.float32(-1e30))
    block_top = jnp.max(masked, axis=2)
    expo_f = jnp.where(is_valid, jnp.exp(masked - block_top[:, :, None]), jnp.float32(0.0))
    block_total = jnp.sum(expo_f, axis=2)
    weighted = jnp.einsum(
        "sqk,skl->sql",
        expo_f.astype(jnp.bfloat16),
        kv_cache[:, :, :latent_width],
        preferred_element_type=jnp.float32,
    )
    stats = jnp.stack([block_top, block_total]).reshape(-1, slice_width)
    sum_slices = [
        weighted[:, :, j * slice_width:(j + 1) * slice_width].reshape(-1, slice_width)
        for j in range(n_ctx)
    ]

    def to_bf16_grid(x):
        return lax.reduce_precision(x, exponent_bits=8, mantissa_bits=7)

    hi = to_bf16_grid(stats)
    mid = to_bf16_grid(stats - hi)
    stats_hi = hi.astype(jnp.bfloat16)
    stats_mid = mid.astype(jnp.bfloat16)
    stats_lo = ((stats - hi) - mid).astype(jnp.bfloat16)
    stat_rows = stats.shape[0]

    def packed_for(target):
        return jnp.concatenate(
            [pick(target, sum_slices).astype(jnp.bfloat16), stats_hi, stats_mid, stats_lo], axis=0
        )

    def unpack(p):
        split = seq_count * q_rows
        f = p[split:].astype(jnp.float32)
        whole = (f[:stat_rows] + f[stat_rows:2 * stat_rows]) + f[2 * stat_rows:]
        return p[:split].astype(jnp.float32), whole

    def combine_blocks(parts):
        sums = [a.reshape(seq_count, q_rows, slice_width) for a, _ in parts]
        st = [b.reshape(2, seq_count, q_rows) for _, b in parts]
        row_top = functools.reduce(jnp.maximum, [t[0] for t in st])
        factors = [jnp.exp(t[0] - row_top) for t in st]
        total = sum(f * t[1] for f, t in zip(factors, st))
        acc = sum(f[:, :, None] * a for f, a in zip(factors, sums))
        return (acc / total[:, :, None]).astype(jnp.bfloat16)

    if small_ctx:
        parts = [(pick(me_ctx, sum_slices), stats)] + [
            unpack(lax.ppermute(packed_for((me_ctx + k) % n_ctx), "ctx", shift_pairs(n_ctx, k)))
            for k in range(1, n_ctx)
        ]
    else:
        packed = jnp.stack([jnp.concatenate([s, stats], axis=0) for s in sum_slices])
        got = lax.all_to_all(packed, "ctx", 0, 0, tiled=False)
        split = seq_count * q_rows
        parts = [(got[j][:split], got[j][split:]) for j in range(n_ctx)]
    latent_out = combine_blocks(parts).reshape(row_count, head_count, slice_width)

    value_part = jnp.einsum("rhl,hlv->rhv", latent_out, w_value, preferred_element_type=jnp.float32)
    if small_ctx:
        sent = value_part.astype(jnp.bfloat16)
        received = [value_part] + [
            lax.ppermute(sent, "ctx", shift_pairs(n_ctx, k)).astype(jnp.float32)
            for k in range(1, n_ctx)
        ]
        values = sum(received).astype(jnp.bfloat16)
    else:
        values = lax.psum(value_part, "ctx").astype(jnp.bfloat16)
    partial_value = jnp.dot(
        values.reshape(row_count, -1), w_output, preferred_element_type=jnp.float32
    )
    if n_head > PERMUTE_MAX:
        return lax.psum_scatter(partial_value, "head", scatter_dimension=1, tiled=True)
    me_head = lax.axis_index("head")
    out_width = partial_value.shape[1] // n_head
    col_slices = [partial_value[:, j * out_width:(j + 1) * out_width] for j in range(n_head)]
    total = pick(me_head, col_slices)
    for k in range(1, n_head):
        total = total + lax.ppermute(
            pick((me_head + k) % n_head, col_slices), "head", shift_pairs(n_head, k)
        )
    return total


def solution(mesh):
    return jax.shard_map(
        functools.partial(per_device, mesh.shape["ctx"], mesh.shape["head"]),
        mesh=mesh,
        in_specs=(
            P("groups", "head", None),
            P("groups", "head", None),
            P("groups", "ctx", None),
            P("groups"),
            P("head", None, "ctx"),
            P("head", "ctx", None),
            P("head", "ctx"),
        ),
        out_specs=P("groups", ("ctx", "head")),
        check_vma=False,
    )
```

```python
import functools

import jax
import jax.numpy as jnp
from jax import lax
from jax.sharding import PartitionSpec as P

ROTARY_CHANNELS = 64
PLAIN_CHANNELS = 128
DRAFT = 2
PERMUTE_MAX = 8


def shift_pairs(n, k):
    return [(i, (i + k) % n) for i in range(n)]


def pick(index, options):
    chosen = options[-1]
    for j in range(len(options) - 2, -1, -1):
        chosen = jnp.where(index == j, options[j], chosen)
    return chosen


def per_device(n_ctx, n_head, query_nope, query_rope, kv_cache, lengths, w_absorb, w_value, w_output):
    seq_count, ctx_rows, channels = kv_cache.shape
    row_count, head_count = query_nope.shape[:2]
    latent_width = channels - query_rope.shape[2]
    slice_width = w_value.shape[1]
    small_ctx = n_ctx <= PERMUTE_MAX
    me_ctx = lax.axis_index("ctx")

    q_part = jnp.einsum(
        "rhn,hnl->rhl", query_nope, w_absorb, preferred_element_type=jnp.float32
    ).astype(jnp.bfloat16)
    if small_ctx:
        received = [q_part] + [
            lax.ppermute(q_part, "ctx", shift_pairs(n_ctx, k)) for k in range(1, n_ctx)
        ]
        kv_blocks = kv_cache[:, :, :latent_width].reshape(seq_count, ctx_rows, n_ctx, -1)
        latent_scores = 0
        for k in range(n_ctx):
            block = lax.dynamic_index_in_dim(kv_blocks, (me_ctx - k) % n_ctx, axis=2, keepdims=False)
            latent_scores = latent_scores + jnp.einsum(
                "sqc,skc->sqk",
                received[k].reshape(seq_count, DRAFT * head_count, -1),
                block,
                preferred_element_type=jnp.float32,
            )
    else:
        q_latent = lax.all_gather(q_part, "ctx", axis=2, tiled=True)
        latent_scores = jnp.einsum(
            "sqc,skc->sqk",
            q_latent.reshape(seq_count, DRAFT * head_count, latent_width),
            kv_cache[:, :, :latent_width],
            preferred_element_type=jnp.float32,
        )
    q_rows = DRAFT * head_count
    rope_scores = jnp.einsum(
        "sqc,skc->sqk",
        query_rope.reshape(seq_count, q_rows, channels - latent_width),
        kv_cache[:, :, latent_width:],
        preferred_element_type=jnp.float32,
    )
    logit_scores = (latent_scores + rope_scores) * (PLAIN_CHANNELS + ROTARY_CHANNELS) ** (-0.5)
    position = me_ctx * ctx_rows + jnp.arange(ctx_rows, dtype=jnp.int32)
    draft_index = jnp.arange(DRAFT * head_count, dtype=jnp.int32) // head_count
    row_limit = lengths[:, None] - DRAFT + draft_index[None, :]
    is_valid = position[None, None, :] <= row_limit[:, :, None]
    masked = jnp.where(is_valid, logit_scores, jnp.float32(-1e30))
    block_top = jnp.max(masked, axis=2)
    expo_f = jnp.where(is_valid, jnp.exp(masked - block_top[:, :, None]), jnp.float32(0.0))
    block_total = jnp.sum(expo_f, axis=2)
    weighted = jnp.einsum(
        "sqk,skl->sql",
        expo_f.astype(jnp.bfloat16),
        kv_cache[:, :, :latent_width],
        preferred_element_type=jnp.float32,
    )
    stats = jnp.stack([block_top, block_total]).reshape(-1, slice_width)
    sum_slices = [
        weighted[:, :, j * slice_width:(j + 1) * slice_width].reshape(-1, slice_width)
        for j in range(n_ctx)
    ]

    def to_bf16_grid(x):
        return lax.reduce_precision(x, exponent_bits=8, mantissa_bits=7)

    hi = to_bf16_grid(stats)
    mid = to_bf16_grid(stats - hi)
    stats_hi = hi.astype(jnp.bfloat16)
    stats_mid = mid.astype(jnp.bfloat16)
    stats_lo = ((stats - hi) - mid).astype(jnp.bfloat16)
    stat_rows = stats.shape[0]

    def packed_for(target):
        return jnp.concatenate(
            [pick(target, sum_slices).astype(jnp.bfloat16), stats_hi, stats_mid, stats_lo], axis=0
        )

    def unpack(p):
        split = seq_count * q_rows
        f = p[split:].astype(jnp.float32)
        whole = (f[:stat_rows] + f[stat_rows:2 * stat_rows]) + f[2 * stat_rows:]
        return p[:split].astype(jnp.float32), whole

    def combine_blocks(parts):
        sums = [a.reshape(seq_count, q_rows, slice_width) for a, _ in parts]
        st = [b.reshape(2, seq_count, q_rows) for _, b in parts]
        row_top = functools.reduce(jnp.maximum, [t[0] for t in st])
        factors = [jnp.exp(t[0] - row_top) for t in st]
        total = sum(f * t[1] for f, t in zip(factors, st))
        acc = sum(f[:, :, None] * a for f, a in zip(factors, sums))
        return (acc / total[:, :, None]).astype(jnp.bfloat16)

    if small_ctx:
        parts = [(pick(me_ctx, sum_slices), stats)] + [
            unpack(lax.ppermute(packed_for((me_ctx + k) % n_ctx), "ctx", shift_pairs(n_ctx, k)))
            for k in range(1, n_ctx)
        ]
    else:
        packed = jnp.stack([jnp.concatenate([s, stats], axis=0) for s in sum_slices])
        got = lax.all_to_all(packed, "ctx", 0, 0, tiled=False)
        split = seq_count * q_rows
        parts = [(got[j][:split], got[j][split:]) for j in range(n_ctx)]
    latent_out = combine_blocks(parts).reshape(row_count, head_count, slice_width)

    value_part = jnp.einsum("rhl,hlv->rhv", latent_out, w_value, preferred_element_type=jnp.float32)
    if small_ctx:
        sent = value_part.astype(jnp.bfloat16)
        received = [value_part] + [
            lax.ppermute(sent, "ctx", shift_pairs(n_ctx, k)).astype(jnp.float32)
            for k in range(1, n_ctx)
        ]
        values = sum(received).astype(jnp.bfloat16)
    else:
        values = lax.psum(value_part, "ctx").astype(jnp.bfloat16)
    partial_value = jnp.dot(
        values.reshape(row_count, -1), w_output, preferred_element_type=jnp.float32
    )
    if n_head > PERMUTE_MAX:
        return lax.psum_scatter(partial_value, "head", scatter_dimension=1, tiled=True)
    me_head = lax.axis_index("head")
    out_width = partial_value.shape[1] // n_head
    col_slices = [partial_value[:, j * out_width:(j + 1) * out_width] for j in range(n_head)]
    total = pick(me_head, col_slices)
    for k in range(1, n_head):
        total = total + lax.ppermute(
            pick((me_head + k) % n_head, col_slices), "head", shift_pairs(n_head, k)
        )
    return total


def solution(mesh):
    return jax.shard_map(
        functools.partial(per_device, mesh.shape["ctx"], mesh.shape["head"]),
        mesh=mesh,
        in_specs=(
            P("groups", "head", None),
            P("groups", "head", None),
            P("groups", "ctx", None),
            P("groups"),
            P("head", None, "ctx"),
            P("head", "ctx", None),
            P("head", "ctx"),
        ),
        out_specs=P("groups", ("ctx", "head")),
        check_vma=False,
    )
```

```python
import functools

import jax
import jax.numpy as jnp
from jax import lax
from jax.experimental.layout import Layout, with_layout_constraint
from jax.sharding import PartitionSpec as P

ROTARY_CHANNELS = 64
PLAIN_CHANNELS = 128
DRAFT = 2
PERMUTE_MAX = 8


def shift_pairs(n, k):
    return [(i, (i + k) % n) for i in range(n)]


def pick(index, options):
    chosen = options[-1]
    for j in range(len(options) - 2, -1, -1):
        chosen = jnp.where(index == j, options[j], chosen)
    return chosen


def per_device(n_ctx, n_head, query_nope, query_rope, kv_cache, lengths, w_absorb, w_value, w_output):
    seq_count, ctx_rows, channels = kv_cache.shape
    row_count, head_count = query_nope.shape[:2]
    latent_width = channels - query_rope.shape[2]
    slice_width = w_value.shape[1]
    small_ctx = n_ctx <= PERMUTE_MAX
    me_ctx = lax.axis_index("ctx")

    q_part = jnp.einsum(
        "rhn,hnl->rhl", query_nope, w_absorb, preferred_element_type=jnp.float32
    ).astype(jnp.bfloat16)
    q_part = with_layout_constraint(q_part, Layout(major_to_minor=(0, 1, 2)))
    if small_ctx:
        received = [q_part] + [
            lax.ppermute(q_part, "ctx", shift_pairs(n_ctx, k)) for k in range(1, n_ctx)
        ]
        source = (me_ctx - jnp.arange(n_ctx, dtype=jnp.int32)[None, None, :, None]) % n_ctx
        q_slots = received[-1][:, :, None, :]
        for k in range(n_ctx - 2, -1, -1):
            q_slots = jnp.where(source == k, received[k][:, :, None, :], q_slots)
        q_latent = q_slots.reshape(row_count, head_count, latent_width)
    else:
        q_latent = lax.all_gather(q_part, "ctx", axis=2, tiled=True)
    q_rows = DRAFT * head_count
    latent_scores = jnp.einsum(
        "sqc,skc->sqk",
        q_latent.reshape(seq_count, q_rows, latent_width),
        kv_cache[:, :, :latent_width],
        preferred_element_type=jnp.float32,
    )
    rope_scores = jnp.einsum(
        "sqc,skc->sqk",
        query_rope.reshape(seq_count, q_rows, channels - latent_width),
        kv_cache[:, :, latent_width:],
        preferred_element_type=jnp.float32,
    )
    logit_scores = (latent_scores + rope_scores) * (PLAIN_CHANNELS + ROTARY_CHANNELS) ** (-0.5)
    position = me_ctx * ctx_rows + jnp.arange(ctx_rows, dtype=jnp.int32)
    draft_index = jnp.arange(DRAFT * head_count, dtype=jnp.int32) // head_count
    row_limit = lengths[:, None] - DRAFT + draft_index[None, :]
    is_valid = position[None, None, :] <= row_limit[:, :, None]
    masked = jnp.where(is_valid, logit_scores, jnp.float32(-1e30))
    block_top = jnp.max(masked, axis=2)
    expo_f = jnp.where(is_valid, jnp.exp(masked - block_top[:, :, None]), jnp.float32(0.0))
    block_total = jnp.sum(expo_f, axis=2)
    weighted = jnp.einsum(
        "sqk,skl->sql",
        expo_f.astype(jnp.bfloat16),
        kv_cache[:, :, :latent_width],
        preferred_element_type=jnp.float32,
    )
    stats = jnp.stack([block_top, block_total]).reshape(-1, slice_width)
    sum_slices = [
        weighted[:, :, j * slice_width:(j + 1) * slice_width].reshape(-1, slice_width)
        for j in range(n_ctx)
    ]

    def to_bf16_grid(x):
        return lax.reduce_precision(x, exponent_bits=8, mantissa_bits=7)

    hi = to_bf16_grid(stats)
    mid = to_bf16_grid(stats - hi)
    stats_hi = hi.astype(jnp.bfloat16)
    stats_mid = mid.astype(jnp.bfloat16)
    stats_lo = ((stats - hi) - mid).astype(jnp.bfloat16)
    stat_rows = stats.shape[0]

    def packed_for(target):
        return jnp.concatenate(
            [pick(target, sum_slices).astype(jnp.bfloat16), stats_hi, stats_mid, stats_lo], axis=0
        )

    def unpack(p):
        split = seq_count * q_rows
        f = p[split:].astype(jnp.float32)
        whole = (f[:stat_rows] + f[stat_rows:2 * stat_rows]) + f[2 * stat_rows:]
        return p[:split].astype(jnp.float32), whole

    def combine_blocks(parts):
        sums = [a.reshape(seq_count, q_rows, slice_width) for a, _ in parts]
        st = [b.reshape(2, seq_count, q_rows) for _, b in parts]
        row_top = functools.reduce(jnp.maximum, [t[0] for t in st])
        factors = [jnp.exp(t[0] - row_top) for t in st]
        total = sum(f * t[1] for f, t in zip(factors, st))
        acc = sum(f[:, :, None] * a for f, a in zip(factors, sums))
        return (acc / total[:, :, None]).astype(jnp.bfloat16)

    if small_ctx:
        parts = [(pick(me_ctx, sum_slices), stats)] + [
            unpack(lax.ppermute(packed_for((me_ctx + k) % n_ctx), "ctx", shift_pairs(n_ctx, k)))
            for k in range(1, n_ctx)
        ]
    else:
        packed = jnp.stack([jnp.concatenate([s, stats], axis=0) for s in sum_slices])
        got = lax.all_to_all(packed, "ctx", 0, 0, tiled=False)
        split = seq_count * q_rows
        parts = [(got[j][:split], got[j][split:]) for j in range(n_ctx)]
    latent_out = combine_blocks(parts).reshape(row_count, head_count, slice_width)

    value_part = jnp.einsum("rhl,hlv->rhv", latent_out, w_value, preferred_element_type=jnp.float32)
    if small_ctx:
        sent = value_part.astype(jnp.bfloat16)
        received = [value_part] + [
            lax.ppermute(sent, "ctx", shift_pairs(n_ctx, k)).astype(jnp.float32)
            for k in range(1, n_ctx)
        ]
        values = sum(received).astype(jnp.bfloat16)
    else:
        values = lax.psum(value_part, "ctx").astype(jnp.bfloat16)
    partial_value = jnp.dot(
        values.reshape(row_count, -1), w_output, preferred_element_type=jnp.float32
    )
    if n_head > PERMUTE_MAX:
        return lax.psum_scatter(partial_value, "head", scatter_dimension=1, tiled=True)
    me_head = lax.axis_index("head")
    out_width = partial_value.shape[1] // n_head
    col_slices = [partial_value[:, j * out_width:(j + 1) * out_width] for j in range(n_head)]
    total = pick(me_head, col_slices)
    for k in range(1, n_head):
        total = total + lax.ppermute(
            pick((me_head + k) % n_head, col_slices), "head", shift_pairs(n_head, k)
        )
    return total


def solution(mesh):
    return jax.shard_map(
        functools.partial(per_device, mesh.shape["ctx"], mesh.shape["head"]),
        mesh=mesh,
        in_specs=(
            P("groups", "head", None),
            P("groups", "head", None),
            P("groups", "ctx", None),
            P("groups"),
            P("head", None, "ctx"),
            P("head", "ctx", None),
            P("head", "ctx"),
        ),
        out_specs=P("groups", ("ctx", "head")),
        check_vma=False,
    )
```

```python
import functools

import jax
import jax.numpy as jnp
from jax import lax
from jax.sharding import PartitionSpec as P

ROTARY_CHANNELS = 64
PLAIN_CHANNELS = 128
DRAFT = 2
PERMUTE_MAX = 8


def shift_pairs(n, k):
    return [(i, (i + k) % n) for i in range(n)]


def shift_order(n):
    return sorted(range(1, n), key=lambda k: -max(k, n - k))


def pick(index, options):
    chosen = options[-1]
    for j in range(len(options) - 2, -1, -1):
        chosen = jnp.where(index == j, options[j], chosen)
    return chosen


def per_device(n_ctx, n_head, query_nope, query_rope, kv_cache, lengths, w_absorb, w_value, w_output):
    seq_count, ctx_rows, channels = kv_cache.shape
    row_count, head_count = query_nope.shape[:2]
    latent_width = channels - query_rope.shape[2]
    slice_width = w_value.shape[1]
    small_ctx = n_ctx <= PERMUTE_MAX
    me_ctx = lax.axis_index("ctx")

    q_part = jnp.einsum(
        "rhn,hnl->rhl", query_nope, w_absorb, preferred_element_type=jnp.float32
    ).astype(jnp.bfloat16)
    if small_ctx:
        received = [q_part] * n_ctx
        for k in shift_order(n_ctx):
            received[k] = lax.ppermute(q_part, "ctx", shift_pairs(n_ctx, k))
        source = (me_ctx - jnp.arange(n_ctx, dtype=jnp.int32)[None, None, :, None]) % n_ctx
        q_slots = received[-1][:, :, None, :]
        for k in range(n_ctx - 2, -1, -1):
            q_slots = jnp.where(source == k, received[k][:, :, None, :], q_slots)
        q_latent = q_slots.reshape(row_count, head_count, latent_width)
    else:
        q_latent = lax.all_gather(q_part, "ctx", axis=2, tiled=True)
    q_rows = DRAFT * head_count
    latent_scores = jnp.einsum(
        "sqc,skc->sqk",
        q_latent.reshape(seq_count, q_rows, latent_width),
        kv_cache[:, :, :latent_width],
        preferred_element_type=jnp.float32,
    )
    rope_scores = jnp.einsum(
        "sqc,skc->sqk",
        query_rope.reshape(seq_count, q_rows, channels - latent_width),
        kv_cache[:, :, latent_width:],
        preferred_element_type=jnp.float32,
    )
    logit_scores = (latent_scores + rope_scores) * (PLAIN_CHANNELS + ROTARY_CHANNELS) ** (-0.5)
    position = me_ctx * ctx_rows + jnp.arange(ctx_rows, dtype=jnp.int32)
    draft_index = jnp.arange(DRAFT * head_count, dtype=jnp.int32) // head_count
    row_limit = lengths[:, None] - DRAFT + draft_index[None, :]
    is_valid = position[None, None, :] <= row_limit[:, :, None]
    masked = jnp.where(is_valid, logit_scores, jnp.float32(-1e30))
    block_top = jnp.max(masked, axis=2)
    expo_f = jnp.where(is_valid, jnp.exp(masked - block_top[:, :, None]), jnp.float32(0.0))
    block_total = jnp.sum(expo_f, axis=2)
    weighted = jnp.einsum(
        "sqk,skl->sql",
        expo_f.astype(jnp.bfloat16),
        kv_cache[:, :, :latent_width],
        preferred_element_type=jnp.float32,
    )
    stats = jnp.stack([block_top, block_total]).reshape(-1, slice_width)
    sum_slices = [
        weighted[:, :, j * slice_width:(j + 1) * slice_width].reshape(-1, slice_width)
        for j in range(n_ctx)
    ]

    def to_bf16_grid(x):
        return lax.reduce_precision(x, exponent_bits=8, mantissa_bits=7)

    hi = to_bf16_grid(stats)
    mid = to_bf16_grid(stats - hi)
    stats_hi = hi.astype(jnp.bfloat16)
    stats_mid = mid.astype(jnp.bfloat16)
    stats_lo = ((stats - hi) - mid).astype(jnp.bfloat16)
    stat_rows = stats.shape[0]

    def packed_for(target):
        return jnp.concatenate(
            [pick(target, sum_slices).astype(jnp.bfloat16), stats_hi, stats_mid, stats_lo], axis=0
        )

    def unpack(p):
        split = seq_count * q_rows
        f = p[split:].astype(jnp.float32)
        whole = (f[:stat_rows] + f[stat_rows:2 * stat_rows]) + f[2 * stat_rows:]
        return p[:split].astype(jnp.float32), whole

    def combine_blocks(parts):
        sums = [a.reshape(seq_count, q_rows, slice_width) for a, _ in parts]
        st = [b.reshape(2, seq_count, q_rows) for _, b in parts]
        row_top = functools.reduce(jnp.maximum, [t[0] for t in st])
        factors = [jnp.exp(t[0] - row_top) for t in st]
        total = sum(f * t[1] for f, t in zip(factors, st))
        acc = sum(f[:, :, None] * a for f, a in zip(factors, sums))
        return (acc / total[:, :, None]).astype(jnp.bfloat16)

    if small_ctx:
        parts = [(pick(me_ctx, sum_slices), stats)] + [
            unpack(lax.ppermute(packed_for((me_ctx + k) % n_ctx), "ctx", shift_pairs(n_ctx, k)))
            for k in shift_order(n_ctx)
        ]
    else:
        packed = jnp.stack([jnp.concatenate([s, stats], axis=0) for s in sum_slices])
        got = lax.all_to_all(packed, "ctx", 0, 0, tiled=False)
        split = seq_count * q_rows
        parts = [(got[j][:split], got[j][split:]) for j in range(n_ctx)]
    latent_out = combine_blocks(parts).reshape(row_count, head_count, slice_width)

    value_part = jnp.einsum("rhl,hlv->rhv", latent_out, w_value, preferred_element_type=jnp.float32)
    if small_ctx:
        sent = value_part.astype(jnp.bfloat16)
        received = [value_part] + [
            lax.ppermute(sent, "ctx", shift_pairs(n_ctx, k)).astype(jnp.float32)
            for k in shift_order(n_ctx)
        ]
        values = sum(received).astype(jnp.bfloat16)
    else:
        values = lax.psum(value_part, "ctx").astype(jnp.bfloat16)
    partial_value = jnp.dot(
        values.reshape(row_count, -1), w_output, preferred_element_type=jnp.float32
    )
    if n_head > PERMUTE_MAX:
        return lax.psum_scatter(partial_value, "head", scatter_dimension=1, tiled=True)
    me_head = lax.axis_index("head")
    out_width = partial_value.shape[1] // n_head
    col_slices = [partial_value[:, j * out_width:(j + 1) * out_width] for j in range(n_head)]
    total = pick(me_head, col_slices)
    for k in range(1, n_head):
        total = total + lax.ppermute(
            pick((me_head + k) % n_head, col_slices), "head", shift_pairs(n_head, k)
        )
    return total


def solution(mesh):
    return jax.shard_map(
        functools.partial(per_device, mesh.shape["ctx"], mesh.shape["head"]),
        mesh=mesh,
        in_specs=(
            P("groups", "head", None),
            P("groups", "head", None),
            P("groups", "ctx", None),
            P("groups"),
            P("head", None, "ctx"),
            P("head", "ctx", None),
            P("head", "ctx"),
        ),
        out_specs=P("groups", ("ctx", "head")),
        check_vma=False,
    )
```

```python
import functools

import jax
import jax.numpy as jnp
from jax import lax
from jax.experimental.layout import Layout, with_layout_constraint
from jax.sharding import PartitionSpec as P

ROTARY_CHANNELS = 64
PLAIN_CHANNELS = 128
DRAFT = 2
PERMUTE_MAX = 8


def shift_pairs(n, k):
    return [(i, (i + k) % n) for i in range(n)]


def pick(index, options):
    chosen = options[-1]
    for j in range(len(options) - 2, -1, -1):
        chosen = jnp.where(index == j, options[j], chosen)
    return chosen


def per_device(n_ctx, n_head, query_nope, query_rope, kv_cache, lengths, w_absorb, w_value, w_output):
    seq_count, ctx_rows, channels = kv_cache.shape
    row_count, head_count = query_nope.shape[:2]
    latent_width = channels - query_rope.shape[2]
    slice_width = w_value.shape[1]
    small_ctx = n_ctx <= PERMUTE_MAX
    me_ctx = lax.axis_index("ctx")

    q_part = jnp.einsum(
        "rhn,hnl->rhl", query_nope, w_absorb, preferred_element_type=jnp.float32
    ).astype(jnp.bfloat16)
    q_part = with_layout_constraint(q_part, Layout(major_to_minor=(0, 1, 2)))
    if small_ctx:
        received = [q_part] + [
            lax.ppermute(q_part, "ctx", shift_pairs(n_ctx, k)) for k in range(1, n_ctx)
        ]
        latent_scores = 0
        for j in range(n_ctx):
            latent_scores = latent_scores + jnp.einsum(
                "sqc,skc->sqk",
                pick((me_ctx - j) % n_ctx, received).reshape(seq_count, DRAFT * head_count, -1),
                kv_cache[:, :, j * slice_width:(j + 1) * slice_width],
                preferred_element_type=jnp.float32,
            )
    else:
        q_latent = lax.all_gather(q_part, "ctx", axis=2, tiled=True)
        latent_scores = jnp.einsum(
            "sqc,skc->sqk",
            q_latent.reshape(seq_count, DRAFT * head_count, latent_width),
            kv_cache[:, :, :latent_width],
            preferred_element_type=jnp.float32,
        )
    q_rows = DRAFT * head_count
    rope_scores = jnp.einsum(
        "sqc,skc->sqk",
        query_rope.reshape(seq_count, q_rows, channels - latent_width),
        kv_cache[:, :, latent_width:],
        preferred_element_type=jnp.float32,
    )
    logit_scores = (latent_scores + rope_scores) * (PLAIN_CHANNELS + ROTARY_CHANNELS) ** (-0.5)
    position = me_ctx * ctx_rows + jnp.arange(ctx_rows, dtype=jnp.int32)
    draft_index = jnp.arange(DRAFT * head_count, dtype=jnp.int32) // head_count
    row_limit = lengths[:, None] - DRAFT + draft_index[None, :]
    is_valid = position[None, None, :] <= row_limit[:, :, None]
    masked = jnp.where(is_valid, logit_scores, jnp.float32(-1e30))
    block_top = jnp.max(masked, axis=2)
    expo_f = jnp.where(is_valid, jnp.exp(masked - block_top[:, :, None]), jnp.float32(0.0))
    block_total = jnp.sum(expo_f, axis=2)
    weighted = jnp.einsum(
        "sqk,skl->sql",
        expo_f.astype(jnp.bfloat16),
        kv_cache[:, :, :latent_width],
        preferred_element_type=jnp.float32,
    )
    stats = jnp.stack([block_top, block_total]).reshape(-1, slice_width)
    sum_slices = [
        weighted[:, :, j * slice_width:(j + 1) * slice_width].reshape(-1, slice_width)
        for j in range(n_ctx)
    ]

    def to_bf16_grid(x):
        return lax.reduce_precision(x, exponent_bits=8, mantissa_bits=7)

    hi = to_bf16_grid(stats)
    mid = to_bf16_grid(stats - hi)
    stats_hi = hi.astype(jnp.bfloat16)
    stats_mid = mid.astype(jnp.bfloat16)
    stats_lo = ((stats - hi) - mid).astype(jnp.bfloat16)
    stat_rows = stats.shape[0]

    def packed_for(target):
        return jnp.concatenate(
            [pick(target, sum_slices).astype(jnp.bfloat16), stats_hi, stats_mid, stats_lo], axis=0
        )

    def unpack(p):
        split = seq_count * q_rows
        f = p[split:].astype(jnp.float32)
        whole = (f[:stat_rows] + f[stat_rows:2 * stat_rows]) + f[2 * stat_rows:]
        return p[:split].astype(jnp.float32), whole

    def combine_blocks(parts):
        sums = [a.reshape(seq_count, q_rows, slice_width) for a, _ in parts]
        st = [b.reshape(2, seq_count, q_rows) for _, b in parts]
        row_top = functools.reduce(jnp.maximum, [t[0] for t in st])
        factors = [jnp.exp(t[0] - row_top) for t in st]
        total = sum(f * t[1] for f, t in zip(factors, st))
        acc = sum(f[:, :, None] * a for f, a in zip(factors, sums))
        return (acc / total[:, :, None]).astype(jnp.bfloat16)

    if small_ctx:
        parts = [(pick(me_ctx, sum_slices), stats)] + [
            unpack(lax.ppermute(packed_for((me_ctx + k) % n_ctx), "ctx", shift_pairs(n_ctx, k)))
            for k in range(1, n_ctx)
        ]
    else:
        packed = jnp.stack([jnp.concatenate([s, stats], axis=0) for s in sum_slices])
        got = lax.all_to_all(packed, "ctx", 0, 0, tiled=False)
        split = seq_count * q_rows
        parts = [(got[j][:split], got[j][split:]) for j in range(n_ctx)]
    latent_out = combine_blocks(parts).reshape(row_count, head_count, slice_width)

    value_part = jnp.einsum("rhl,hlv->rhv", latent_out, w_value, preferred_element_type=jnp.float32)
    if small_ctx:
        sent = value_part.astype(jnp.bfloat16)
        received = [value_part] + [
            lax.ppermute(sent, "ctx", shift_pairs(n_ctx, k)).astype(jnp.float32)
            for k in range(1, n_ctx)
        ]
        values = sum(received).astype(jnp.bfloat16)
    else:
        values = lax.psum(value_part, "ctx").astype(jnp.bfloat16)
    partial_value = jnp.dot(
        values.reshape(row_count, -1), w_output, preferred_element_type=jnp.float32
    )
    if n_head > PERMUTE_MAX:
        return lax.psum_scatter(partial_value, "head", scatter_dimension=1, tiled=True)
    me_head = lax.axis_index("head")
    out_width = partial_value.shape[1] // n_head
    col_slices = [partial_value[:, j * out_width:(j + 1) * out_width] for j in range(n_head)]
    total = pick(me_head, col_slices)
    for k in range(1, n_head):
        total = total + lax.ppermute(
            pick((me_head + k) % n_head, col_slices), "head", shift_pairs(n_head, k)
        )
    return total


def solution(mesh):
    return jax.shard_map(
        functools.partial(per_device, mesh.shape["ctx"], mesh.shape["head"]),
        mesh=mesh,
        in_specs=(
            P("groups", "head", None),
            P("groups", "head", None),
            P("groups", "ctx", None),
            P("groups"),
            P("head", None, "ctx"),
            P("head", "ctx", None),
            P("head", "ctx"),
        ),
        out_specs=P("groups", ("ctx", "head")),
        check_vma=False,
    )
```

```python
import functools

import jax
import jax.numpy as jnp
from jax import lax
from jax.sharding import PartitionSpec as P

ROTARY_CHANNELS = 64
PLAIN_CHANNELS = 128
DRAFT = 2
PERMUTE_MAX = 8


def shift_pairs(n, k):
    return [(i, (i + k) % n) for i in range(n)]


def pick(index, options):
    chosen = options[-1]
    for j in range(len(options) - 2, -1, -1):
        chosen = jnp.where(index == j, options[j], chosen)
    return chosen


def per_device(n_ctx, n_head, query_nope, query_rope, kv_cache, lengths, w_absorb, w_value, w_output):
    seq_count, ctx_rows, channels = kv_cache.shape
    row_count, head_count = query_nope.shape[:2]
    latent_width = channels - query_rope.shape[2]
    slice_width = w_value.shape[1]
    small_ctx = n_ctx <= PERMUTE_MAX
    me_ctx = lax.axis_index("ctx")

    q_part = jnp.einsum(
        "rhn,hnl->rhl", query_nope, w_absorb, preferred_element_type=jnp.float32
    ).astype(jnp.bfloat16)
    if small_ctx:
        received = [q_part] + [
            lax.ppermute(q_part, "ctx", shift_pairs(n_ctx, k)) for k in range(1, n_ctx)
        ]
        source = (me_ctx - jnp.arange(n_ctx, dtype=jnp.int32)[None, None, :, None]) % n_ctx
        q_slots = received[-1][:, :, None, :]
        for k in range(n_ctx - 2, -1, -1):
            q_slots = jnp.where(source == k, received[k][:, :, None, :], q_slots)
        q_latent = q_slots.reshape(row_count, head_count, latent_width)
    else:
        q_latent = lax.all_gather(q_part, "ctx", axis=2, tiled=True)
    q_rows = DRAFT * head_count
    latent_scores = jnp.einsum(
        "sqc,skc->sqk",
        q_latent.reshape(seq_count, q_rows, latent_width),
        kv_cache[:, :, :latent_width],
        preferred_element_type=jnp.float32,
    )
    rope_scores = jnp.einsum(
        "sqc,skc->sqk",
        query_rope.reshape(seq_count, q_rows, channels - latent_width),
        kv_cache[:, :, latent_width:],
        preferred_element_type=jnp.float32,
    )
    logit_scores = (latent_scores + rope_scores) * (PLAIN_CHANNELS + ROTARY_CHANNELS) ** (-0.5)
    position = me_ctx * ctx_rows + jnp.arange(ctx_rows, dtype=jnp.int32)
    draft_index = jnp.arange(DRAFT * head_count, dtype=jnp.int32) // head_count
    row_limit = lengths[:, None] - DRAFT + draft_index[None, :]
    is_valid = position[None, None, :] <= row_limit[:, :, None]
    masked = jnp.where(is_valid, logit_scores, jnp.float32(-1e30))
    block_top = jnp.max(masked, axis=2)
    expo_f = jnp.where(is_valid, jnp.exp(masked - block_top[:, :, None]), jnp.float32(0.0))
    block_total = jnp.sum(expo_f, axis=2)
    weighted = jnp.einsum(
        "sqk,skl->sql",
        expo_f.astype(jnp.bfloat16),
        kv_cache[:, :, :latent_width],
        preferred_element_type=jnp.float32,
    )
    stats = jnp.stack([block_top, block_total]).reshape(-1, slice_width)
    sum_slices = [
        weighted[:, :, j * slice_width:(j + 1) * slice_width].reshape(-1, slice_width)
        for j in range(n_ctx)
    ]

    def to_bf16_grid(x):
        return lax.reduce_precision(x, exponent_bits=8, mantissa_bits=7)

    hi = to_bf16_grid(stats)
    mid = to_bf16_grid(stats - hi)
    stats_hi = hi.astype(jnp.bfloat16)
    stats_mid = mid.astype(jnp.bfloat16)
    stats_lo = ((stats - hi) - mid).astype(jnp.bfloat16)
    stat_rows = stats.shape[0]

    def packed_for(target):
        return jnp.concatenate(
            [pick(target, sum_slices).astype(jnp.bfloat16), stats_hi, stats_mid, stats_lo], axis=0
        )

    def unpack(p):
        split = seq_count * q_rows
        f = p[split:].astype(jnp.float32)
        whole = (f[:stat_rows] + f[stat_rows:2 * stat_rows]) + f[2 * stat_rows:]
        return p[:split].astype(jnp.float32), whole

    def combine_blocks(parts):
        sums = [a.reshape(seq_count, q_rows, slice_width) for a, _ in parts]
        st = [b.reshape(2, seq_count, q_rows) for _, b in parts]
        row_top = functools.reduce(jnp.maximum, [t[0] for t in st])
        factors = [jnp.exp(t[0] - row_top) for t in st]
        total = sum(f * t[1] for f, t in zip(factors, st))
        acc = sum(f[:, :, None] * a for f, a in zip(factors, sums))
        return (acc / total[:, :, None]).astype(jnp.bfloat16)

    if small_ctx:
        parts = [(pick(me_ctx, sum_slices), stats)] + [
            unpack(lax.ppermute(packed_for((me_ctx + k) % n_ctx), "ctx", shift_pairs(n_ctx, k)))
            for k in range(1, n_ctx)
        ]
    else:
        packed = jnp.stack([jnp.concatenate([s, stats], axis=0) for s in sum_slices])
        got = lax.all_to_all(packed, "ctx", 0, 0, tiled=False)
        split = seq_count * q_rows
        parts = [(got[j][:split], got[j][split:]) for j in range(n_ctx)]
    latent_out = combine_blocks(parts).reshape(row_count, head_count, slice_width)

    value_part = jnp.einsum("rhl,hlv->rhv", latent_out, w_value, preferred_element_type=jnp.float32)
    if small_ctx:
        sent = value_part.astype(jnp.bfloat16)
        received = [value_part] + [
            lax.ppermute(sent, "ctx", shift_pairs(n_ctx, k)).astype(jnp.float32)
            for k in range(1, n_ctx)
        ]
        values = sum(received).astype(jnp.bfloat16)
    else:
        values = lax.psum(value_part, "ctx").astype(jnp.bfloat16)
    partial_value = jnp.dot(
        values.reshape(row_count, -1), w_output, preferred_element_type=jnp.float32
    )
    if n_head > PERMUTE_MAX:
        return lax.psum_scatter(partial_value, "head", scatter_dimension=1, tiled=True)
    me_head = lax.axis_index("head")
    out_width = partial_value.shape[1] // n_head
    col_slices = [partial_value[:, j * out_width:(j + 1) * out_width] for j in range(n_head)]
    total = pick(me_head, col_slices)
    if n_head & (n_head - 1) == 0:
        for m in range(1, n_head):
            pairs = [(i, i ^ m) for i in range(n_head)]
            total = total + lax.ppermute(pick(me_head ^ m, col_slices), "head", pairs)
        return total
    for k in range(1, n_head):
        total = total + lax.ppermute(
            pick((me_head + k) % n_head, col_slices), "head", shift_pairs(n_head, k)
        )
    return total


def solution(mesh):
    return jax.shard_map(
        functools.partial(per_device, mesh.shape["ctx"], mesh.shape["head"]),
        mesh=mesh,
        in_specs=(
            P("groups", "head", None),
            P("groups", "head", None),
            P("groups", "ctx", None),
            P("groups"),
            P("head", None, "ctx"),
            P("head", "ctx", None),
            P("head", "ctx"),
        ),
        out_specs=P("groups", ("ctx", "head")),
        check_vma=False,
    )
```

```python
import functools

import jax
import jax.numpy as jnp
from jax import lax
from jax.sharding import PartitionSpec as P

ROTARY_CHANNELS = 64
PLAIN_CHANNELS = 128
DRAFT = 2
PERMUTE_MAX = 8


def shift_pairs(n, k):
    return [(i, (i + k) % n) for i in range(n)]


def pick(index, options):
    chosen = options[-1]
    for j in range(len(options) - 2, -1, -1):
        chosen = jnp.where(index == j, options[j], chosen)
    return chosen


def per_device(n_ctx, n_head, query_nope, query_rope, kv_cache, lengths, w_absorb, w_value, w_output):
    seq_count, ctx_rows, channels = kv_cache.shape
    row_count, head_count = query_nope.shape[:2]
    latent_width = channels - query_rope.shape[2]
    slice_width = w_value.shape[1]
    small_ctx = n_ctx <= PERMUTE_MAX
    me_ctx = lax.axis_index("ctx")

    q_part = jnp.einsum(
        "rhn,hnl->rhl", query_nope, w_absorb, preferred_element_type=jnp.float32
    ).astype(jnp.bfloat16)
    if small_ctx:
        received = [q_part] + [
            lax.ppermute(q_part, "ctx", shift_pairs(n_ctx, k)) for k in range(1, n_ctx)
        ]
        source = (me_ctx - jnp.arange(n_ctx, dtype=jnp.int32)[None, None, :, None]) % n_ctx
        q_slots = received[-1][:, :, None, :]
        for k in range(n_ctx - 2, -1, -1):
            q_slots = jnp.where(source == k, received[k][:, :, None, :], q_slots)
        q_latent = q_slots.reshape(row_count, head_count, latent_width)
    else:
        q_latent = lax.all_gather(q_part, "ctx", axis=2, tiled=True)
    q_rows = DRAFT * head_count
    latent_scores = jnp.einsum(
        "sqc,skc->sqk",
        q_latent.reshape(seq_count, q_rows, latent_width),
        kv_cache[:, :, :latent_width],
        preferred_element_type=jnp.float32,
    )
    rope_scores = jnp.einsum(
        "sqc,skc->sqk",
        query_rope.reshape(seq_count, q_rows, channels - latent_width),
        kv_cache[:, :, latent_width:],
        preferred_element_type=jnp.float32,
    )
    logit_scores = (latent_scores + rope_scores) * (PLAIN_CHANNELS + ROTARY_CHANNELS) ** (-0.5)
    position = me_ctx * ctx_rows + jnp.arange(ctx_rows, dtype=jnp.int32)
    draft_index = jnp.arange(DRAFT * head_count, dtype=jnp.int32) // head_count
    row_limit = lengths[:, None] - DRAFT + draft_index[None, :]
    is_valid = position[None, None, :] <= row_limit[:, :, None]
    masked = jnp.where(is_valid, logit_scores, jnp.float32(-1e30))
    block_top = jnp.max(masked, axis=2)
    expo_f = jnp.where(is_valid, jnp.exp(masked - block_top[:, :, None]), jnp.float32(0.0))
    block_total = jnp.sum(expo_f, axis=2)
    weighted = jnp.einsum(
        "sqk,skl->sql",
        expo_f.astype(jnp.bfloat16),
        kv_cache[:, :, :latent_width],
        preferred_element_type=jnp.float32,
    )
    stats = jnp.stack([block_top, block_total]).reshape(-1, slice_width)
    sum_slices = [
        weighted[:, :, j * slice_width:(j + 1) * slice_width].reshape(-1, slice_width)
        for j in range(n_ctx)
    ]

    def to_bf16_grid(x):
        return lax.reduce_precision(x, exponent_bits=8, mantissa_bits=7)

    hi = to_bf16_grid(stats)
    mid = to_bf16_grid(stats - hi)
    stats_hi = hi.astype(jnp.bfloat16)
    stats_mid = mid.astype(jnp.bfloat16)
    stats_lo = ((stats - hi) - mid).astype(jnp.bfloat16)
    stat_rows = stats.shape[0]

    def packed_for(target):
        return jnp.concatenate(
            [pick(target, sum_slices).astype(jnp.bfloat16), stats_hi, stats_mid, stats_lo], axis=0
        )

    def unpack(p):
        split = seq_count * q_rows
        f = p[split:].astype(jnp.float32)
        whole = (f[:stat_rows] + f[stat_rows:2 * stat_rows]) + f[2 * stat_rows:]
        return p[:split].astype(jnp.float32), whole

    def combine_blocks(parts):
        sums = [a.reshape(seq_count, q_rows, slice_width) for a, _ in parts]
        st = [b.reshape(2, seq_count, q_rows) for _, b in parts]
        row_top = functools.reduce(jnp.maximum, [t[0] for t in st])
        factors = [jnp.exp(t[0] - row_top) for t in st]
        total = sum(f * t[1] for f, t in zip(factors, st))
        acc = sum(f[:, :, None] * a for f, a in zip(factors, sums))
        return (acc / total[:, :, None]).astype(jnp.bfloat16)

    if small_ctx:
        parts = [(pick(me_ctx, sum_slices), stats)] + [
            unpack(lax.ppermute(packed_for((me_ctx + k) % n_ctx), "ctx", shift_pairs(n_ctx, k)))
            for k in range(1, n_ctx)
        ]
    else:
        packed = jnp.stack([jnp.concatenate([s, stats], axis=0) for s in sum_slices])
        got = lax.all_to_all(packed, "ctx", 0, 0, tiled=False)
        split = seq_count * q_rows
        parts = [(got[j][:split], got[j][split:]) for j in range(n_ctx)]
    latent_out = combine_blocks(parts).reshape(row_count, head_count, slice_width)

    value_part = jnp.einsum("rhl,hlv->rhv", latent_out, w_value, preferred_element_type=jnp.float32)
    if small_ctx:
        sent = value_part.astype(jnp.bfloat16)
        received = [value_part] + [
            lax.ppermute(sent, "ctx", shift_pairs(n_ctx, k)).astype(jnp.float32)
            for k in range(1, n_ctx)
        ]
        values = sum(received).astype(jnp.bfloat16)
    else:
        values = lax.psum(value_part, "ctx").astype(jnp.bfloat16)
    partial_value = jnp.dot(
        values.reshape(row_count, -1), w_output, preferred_element_type=jnp.float32
    )
    if n_head > PERMUTE_MAX:
        return lax.psum_scatter(partial_value, "head", scatter_dimension=1, tiled=True)
    me_head = lax.axis_index("head")
    out_width = partial_value.shape[1] // n_head
    col_slices = [partial_value[:, j * out_width:(j + 1) * out_width] for j in range(n_head)]
    total = pick(me_head, col_slices)
    if n_head & (n_head - 1) == 0:
        for m in sorted(range(1, n_head), key=lambda m: (m == 1, -m & 2, m)):
            pairs = [(i, i ^ m) for i in range(n_head)]
            total = total + lax.ppermute(pick(me_head ^ m, col_slices), "head", pairs)
        return total
    for k in range(1, n_head):
        total = total + lax.ppermute(
            pick((me_head + k) % n_head, col_slices), "head", shift_pairs(n_head, k)
        )
    return total


def solution(mesh):
    return jax.shard_map(
        functools.partial(per_device, mesh.shape["ctx"], mesh.shape["head"]),
        mesh=mesh,
        in_specs=(
            P("groups", "head", None),
            P("groups", "head", None),
            P("groups", "ctx", None),
            P("groups"),
            P("head", None, "ctx"),
            P("head", "ctx", None),
            P("head", "ctx"),
        ),
        out_specs=P("groups", ("ctx", "head")),
        check_vma=False,
    )
```

```python
import functools

import jax
import jax.numpy as jnp
from jax import lax
from jax.sharding import PartitionSpec as P

ROTARY_CHANNELS = 64
PLAIN_CHANNELS = 128
DRAFT = 2
PERMUTE_MAX = 8


def shift_pairs(n, k):
    return [(i, (i + k) % n) for i in range(n)]


def pick(index, options):
    chosen = options[-1]
    for j in range(len(options) - 2, -1, -1):
        chosen = jnp.where(index == j, options[j], chosen)
    return chosen


def per_device(n_ctx, n_head, query_nope, query_rope, kv_cache, lengths, w_absorb, w_value, w_output):
    seq_count, ctx_rows, channels = kv_cache.shape
    row_count, head_count = query_nope.shape[:2]
    latent_width = channels - query_rope.shape[2]
    slice_width = w_value.shape[1]
    small_ctx = n_ctx <= PERMUTE_MAX
    me_ctx = lax.axis_index("ctx")

    q_part = jnp.einsum(
        "rhn,hnl->rhl", query_nope, w_absorb, preferred_element_type=jnp.float32
    ).astype(jnp.bfloat16)
    if small_ctx:
        received = [q_part] + [
            lax.ppermute(q_part, "ctx", shift_pairs(n_ctx, k)) for k in range(1, n_ctx)
        ]
        source = (me_ctx - jnp.arange(n_ctx, dtype=jnp.int32)[None, None, :, None]) % n_ctx
        q_slots = received[-1][:, :, None, :]
        for k in range(n_ctx - 2, -1, -1):
            q_slots = jnp.where(source == k, received[k][:, :, None, :], q_slots)
        q_latent = q_slots.reshape(row_count, head_count, latent_width)
    else:
        q_latent = lax.all_gather(q_part, "ctx", axis=2, tiled=True)
    q_rows = DRAFT * head_count
    latent_scores = jnp.einsum(
        "sqc,skc->sqk",
        q_latent.reshape(seq_count, q_rows, latent_width),
        kv_cache[:, :, :latent_width],
        preferred_element_type=jnp.float32,
    )
    rope_scores = jnp.einsum(
        "sqc,skc->sqk",
        query_rope.reshape(seq_count, q_rows, channels - latent_width),
        kv_cache[:, :, latent_width:],
        preferred_element_type=jnp.float32,
    )
    logit_scores = (latent_scores + rope_scores) * (PLAIN_CHANNELS + ROTARY_CHANNELS) ** (-0.5)
    position = me_ctx * ctx_rows + jnp.arange(ctx_rows, dtype=jnp.int32)
    draft_index = jnp.arange(DRAFT * head_count, dtype=jnp.int32) // head_count
    row_limit = lengths[:, None] - DRAFT + draft_index[None, :]
    is_valid = position[None, None, :] <= row_limit[:, :, None]
    masked = jnp.where(is_valid, logit_scores, jnp.float32(-1e30))
    block_top = jnp.max(masked, axis=2)
    expo_f = jnp.where(is_valid, jnp.exp(masked - block_top[:, :, None]), jnp.float32(0.0))
    block_total = jnp.sum(expo_f, axis=2)
    weighted = jnp.einsum(
        "sqk,skl->sql",
        expo_f.astype(jnp.bfloat16),
        kv_cache,
        preferred_element_type=jnp.float32,
    )[:, :, :latent_width]
    stats = jnp.stack([block_top, block_total]).reshape(-1, slice_width)
    sum_slices = [
        weighted[:, :, j * slice_width:(j + 1) * slice_width].reshape(-1, slice_width)
        for j in range(n_ctx)
    ]

    def to_bf16_grid(x):
        return lax.reduce_precision(x, exponent_bits=8, mantissa_bits=7)

    hi = to_bf16_grid(stats)
    mid = to_bf16_grid(stats - hi)
    stats_hi = hi.astype(jnp.bfloat16)
    stats_mid = mid.astype(jnp.bfloat16)
    stats_lo = ((stats - hi) - mid).astype(jnp.bfloat16)
    stat_rows = stats.shape[0]

    def packed_for(target):
        return jnp.concatenate(
            [pick(target, sum_slices).astype(jnp.bfloat16), stats_hi, stats_mid, stats_lo], axis=0
        )

    def unpack(p):
        split = seq_count * q_rows
        f = p[split:].astype(jnp.float32)
        whole = (f[:stat_rows] + f[stat_rows:2 * stat_rows]) + f[2 * stat_rows:]
        return p[:split].astype(jnp.float32), whole

    def combine_blocks(parts):
        sums = [a.reshape(seq_count, q_rows, slice_width) for a, _ in parts]
        st = [b.reshape(2, seq_count, q_rows) for _, b in parts]
        row_top = functools.reduce(jnp.maximum, [t[0] for t in st])
        factors = [jnp.exp(t[0] - row_top) for t in st]
        total = sum(f * t[1] for f, t in zip(factors, st))
        acc = sum(f[:, :, None] * a for f, a in zip(factors, sums))
        return (acc / total[:, :, None]).astype(jnp.bfloat16)

    if small_ctx:
        parts = [(pick(me_ctx, sum_slices), stats)] + [
            unpack(lax.ppermute(packed_for((me_ctx + k) % n_ctx), "ctx", shift_pairs(n_ctx, k)))
            for k in range(1, n_ctx)
        ]
    else:
        packed = jnp.stack([jnp.concatenate([s, stats], axis=0) for s in sum_slices])
        got = lax.all_to_all(packed, "ctx", 0, 0, tiled=False)
        split = seq_count * q_rows
        parts = [(got[j][:split], got[j][split:]) for j in range(n_ctx)]
    latent_out = combine_blocks(parts).reshape(row_count, head_count, slice_width)

    value_part = jnp.einsum("rhl,hlv->rhv", latent_out, w_value, preferred_element_type=jnp.float32)
    if small_ctx:
        sent = value_part.astype(jnp.bfloat16)
        received = [value_part] + [
            lax.ppermute(sent, "ctx", shift_pairs(n_ctx, k)).astype(jnp.float32)
            for k in range(1, n_ctx)
        ]
        values = sum(received).astype(jnp.bfloat16)
    else:
        values = lax.psum(value_part, "ctx").astype(jnp.bfloat16)
    partial_value = jnp.dot(
        values.reshape(row_count, -1), w_output, preferred_element_type=jnp.float32
    )
    if n_head > PERMUTE_MAX:
        return lax.psum_scatter(partial_value, "head", scatter_dimension=1, tiled=True)
    me_head = lax.axis_index("head")
    out_width = partial_value.shape[1] // n_head
    col_slices = [partial_value[:, j * out_width:(j + 1) * out_width] for j in range(n_head)]
    total = pick(me_head, col_slices)
    if n_head & (n_head - 1) == 0:
        for m in sorted(range(1, n_head), key=lambda m: (m == 1, -m & 2, m)):
            pairs = [(i, i ^ m) for i in range(n_head)]
            total = total + lax.ppermute(pick(me_head ^ m, col_slices), "head", pairs)
        return total
    for k in range(1, n_head):
        total = total + lax.ppermute(
            pick((me_head + k) % n_head, col_slices), "head", shift_pairs(n_head, k)
        )
    return total


def solution(mesh):
    return jax.shard_map(
        functools.partial(per_device, mesh.shape["ctx"], mesh.shape["head"]),
        mesh=mesh,
        in_specs=(
            P("groups", "head", None),
            P("groups", "head", None),
            P("groups", "ctx", None),
            P("groups"),
            P("head", None, "ctx"),
            P("head", "ctx", None),
            P("head", "ctx"),
        ),
        out_specs=P("groups", ("ctx", "head")),
        check_vma=False,
    )
```
